512 devices in a mesh: ind: 64 (over z, y), snp: 8 (over x, core).
Axes of the slice: x: 4, y: 8, z: 8, core: 2. Of those that a mesh axis runs over, the one named last changes fastest.
Arguments:
- genotypes: int32 [20480, 4096], P('ind', 'snp'), may hold values from 0 to 2730, as said below
- means: float32 [4096], P('snp'), may hold values from 0.17 to 1.83
- scales: float32 [4096], P('snp'), may hold values from 1.2 to 2.6
- basis_in: bfloat16 [122880, 128], P('ind'), may hold values from -12 to 12
Outputs:
- basis: bfloat16 [122880, 128], P('ind')
- triangle: float32 [128, 128], replicated
The draws below stay inside these ranges and needn't reach their ends.
Inputs may be any that keep to these rules, and one draw needn't show every extreme that they name: `genotypes`: word w of SNP s holds the dosage of individual 6 w + j in bits 2 j and 2 j + 1, j = 0..5; every such field is 0, 1 or 2.
All inputs are finite; a program needn't handle non-finite values.
Results may differ from the reference program's by a relative error of at most 0.0025.
The reference program's roundings to bfloat16 on the way count: a program that leaves them out, or rounds other values in their place, can miss the bound.
Values may be sent and summed in bfloat16 or wider, within the bound.
No kernel may reach another device: no remote copies, remote signals or barrier semaphores. Data moves between devices by JAX's collectives and lax.ppermute only.
A program may use at most 64 MiB of HBM per device.

```python
import math
import jax
import jax.numpy as jnp
from jax import lax

SNPS = 4096
RANK = 128
IND_DEV = 1920
INDS = 122880
WORDS = 20480


def snp_frequency(key):
    return jax.random.randint(jax.random.fold_in(key, 7), (SNPS,), 100, 900)


def cohort_start(key):
    block = jax.random.randint(jax.random.fold_in(key, 31), (), 0, INDS // IND_DEV)
    return block.astype(jnp.int32) * IND_DEV


def draw_genotypes(key, part):
    freq = snp_frequency(key)
    signs = jax.random.randint(jax.random.fold_in(key, 32), (SNPS,), 0, 2) * 2 - 1
    sizes_drift = jax.random.randint(jax.random.fold_in(key, 33), (SNPS,), 200, 350)
    shifted = jnp.clip(freq + signs * sizes_drift, 20, 980)
    start = cohort_start(key)
    cohort = IND_DEV // 8
    shifts = 2 * jnp.arange(6, dtype=jnp.int32)
    base_key = jax.random.fold_in(key, 11)
    places = jnp.arange(160, dtype=jnp.int32)[:, None] * 6 + jnp.arange(6, dtype=jnp.int32)[None, :]

    def one_block(index):
        rows = index.astype(jnp.int32) * 960 + places
        inside = jnp.logical_and(rows >= start, rows < start + cohort)
        level = jnp.where(inside[:, :, None], shifted[None, None, :], freq[None, None, :])
        draws = jax.random.randint(jax.random.fold_in(base_key, index), (160, 6, SNPS), 0, 1000000)
        dose = (draws % 1000 < level).astype(jnp.int32) + (draws // 1000 < level).astype(jnp.int32)
        return jnp.sum(jnp.left_shift(dose, shifts[None, :, None]), axis=1)
    return lax.map(one_block, jnp.arange(WORDS // 160)).reshape(WORDS, SNPS)


def draw_means(key, part):
    freq = snp_frequency(key).astype(jnp.float32)
    offset = jax.random.uniform(jax.random.fold_in(key, 13), (SNPS,), jnp.float32, -0.03, 0.03)
    return 2.0 * freq / 1000.0 + offset


def draw_basis_in(key, part):
    own = jax.random.normal(jax.random.fold_in(key, 21), (INDS, RANK), jnp.float32)
    shared = jax.random.normal(jax.random.fold_in(key, 22), (INDS, 1), jnp.float32)
    column = jnp.exp(jax.random.uniform(jax.random.fold_in(key, 23), (RANK,), jnp.float32, 0.0, math.log(3.0)))
    direction = jax.random.normal(jax.random.fold_in(key, 34), (RANK,), jnp.float32) * (1.0 / math.sqrt(RANK))
    start = cohort_start(key)
    rows = jnp.arange(INDS, dtype=jnp.int32)
    inside = jnp.logical_and(rows >= start, rows < start + IND_DEV // 8)
    lift = jnp.where(inside[:, None], 6.0 * direction[None, :], jnp.zeros((INDS, RANK), jnp.float32))
    values = jnp.clip((own + 0.7 * shared) * column + lift, -12.0, 12.0)
    return values.astype(jnp.bfloat16)


def block_levels(key, dims, shards, low, high):
    gain = 1.0
    for position, shards_of in shards:
        heights = jax.random.uniform(jax.random.fold_in(jax.random.fold_in(key, 6), position), (shards_of,), jnp.float32, low / len(shards), high / len(shards))
        gain = gain * jnp.repeat(jnp.exp(heights), dims[position] // shards_of).reshape((-1,) + (1,) * (len(dims) - 1 - position))
    return gain


def setup_inputs(seed: int = 0) -> dict:
    key_list = jax.random.split(jax.random.key(seed), 5)
    genotypes = draw_genotypes(jax.random.fold_in(key_list[4], 71), 0)
    means = draw_means(jax.random.fold_in(key_list[4], 71), 0)
    scales = jnp.clip(jnp.exp(math.log(2.6) - 0.7731898 * jax.random.uniform(key_list[2], (SNPS,), jnp.float32) ** block_levels(key_list[2], (SNPS,), ((0, 8),), -0.2, 0.2)), 1.2, 2.6)
    basis_in = draw_basis_in(jax.random.fold_in(key_list[4], 71), 0)
    return dict(genotypes=genotypes, means=means, scales=scales, basis_in=basis_in)


def standardize(words, means, scales):
    shifts = 2 * jnp.arange(6, dtype=jnp.int32)
    dose = jnp.bitwise_and(jnp.right_shift(words[:, None, :], shifts[None, :, None]), 3)
    values = (dose.astype(jnp.float32) - means) * scales
    return values.astype(jnp.bfloat16).reshape(words.shape[0] * 6, words.shape[1])

def upper_factor(gram):
    count = gram.shape[0]
    places = jnp.arange(count, dtype=jnp.int32)

    def column(index, lower):
        row_mask = (places == index)[:, None]
        row_here = lax.optimization_barrier(jnp.sum(jnp.where(row_mask, lower, jnp.zeros_like(lower)), axis=0))
        target = lax.optimization_barrier(jnp.sum(jnp.where(places[None, :] == index, gram, jnp.zeros_like(gram)), axis=1))
        reduced = target - jnp.dot(lower, row_here, precision=lax.Precision.HIGHEST)
        pivot = jnp.sum(jnp.where(places == index, reduced, jnp.zeros_like(reduced)))
        values = jnp.where(places >= index, reduced / jnp.sqrt(pivot), jnp.zeros_like(reduced))
        return jnp.where(places[None, :] == index, values[:, None], lower)
    lower = lax.fori_loop(0, count, column, jnp.zeros_like(gram))
    return lower.T

def upper_inverse(upper):
    count = upper.shape[0]
    places = jnp.arange(count, dtype=jnp.int32)

    def row_step(step, solved):
        index = count - 1 - step
        row_mask = (places == index)[:, None]
        row_here = lax.optimization_barrier(jnp.sum(jnp.where(row_mask, upper, jnp.zeros_like(upper)), axis=0))
        pivot = jnp.sum(jnp.where(places == index, row_here, jnp.zeros_like(row_here)))
        unit = jnp.where(places == index, jnp.ones_like(row_here), jnp.zeros_like(row_here))
        values = (unit - jnp.dot(row_here, solved, precision=lax.Precision.HIGHEST)) / pivot
        return jnp.where(row_mask, values[None, :], solved)
    return lax.fori_loop(0, count, row_step, jnp.zeros_like(upper))

def reference(genotypes, means, scales, basis_in):
    blocks = WORDS // 160
    word_blocks = genotypes.reshape(blocks, 160, SNPS)
    row_blocks = basis_in.reshape(blocks, 960, RANK)

    def first(total, pair):
        words, rows = pair
        zeta = standardize(words, means, scales)
        return (total + jnp.dot(zeta.T, rows, preferred_element_type=jnp.float32), None)
    loadings, _ = lax.scan(first, jnp.zeros((SNPS, RANK), jnp.float32), (word_blocks, row_blocks))
    loadings_b = loadings.astype(jnp.bfloat16)

    def second(total, words):
        zeta = standardize(words, means, scales)
        sketch = jnp.dot(zeta, loadings_b, preferred_element_type=jnp.float32)
        gram_part = jnp.dot(sketch.T, sketch, precision=lax.Precision.HIGHEST)
        return (total + gram_part, sketch)
    gram, sketches = lax.scan(second, jnp.zeros((RANK, RANK), jnp.float32), word_blocks)
    sketch_all = sketches.reshape(INDS, RANK)
    upper = upper_factor(gram)
    inverse = upper_inverse(upper)
    basis = (jnp.dot(sketch_all, inverse, precision=lax.Precision.HIGHEST) * math.sqrt(INDS)).astype(jnp.bfloat16)
    triangle = upper / (INDS * math.sqrt(SNPS))
    return (basis, triangle)
```

```python
import math

import jax
import jax.numpy as jnp
from jax import lax
from jax.experimental import pallas as pl
from jax.experimental.pallas import tpu as pltpu
from jax.sharding import Mesh
from jax.sharding import PartitionSpec as P

SNPS = 4096


def standardize(words, means, scales):
    shifts = 2 * jnp.arange(6, dtype=jnp.int32)
    dose = jnp.bitwise_and(jnp.right_shift(words[:, None, :], shifts[None, :, None]), 3)
    values = (dose.astype(jnp.float32) - means) * scales
    return values.astype(jnp.bfloat16).reshape(words.shape[0] * 6, words.shape[1])


def factor_kernel(gram_ref, upper_ref, lower_inv_ref):
    n = gram_ref.shape[0]
    sub = lax.broadcasted_iota(jnp.int32, (n, n), 0)
    lane = lax.broadcasted_iota(jnp.int32, (n, n), 1)
    sub_col = lax.broadcasted_iota(jnp.int32, (n, 1), 0)
    eye = sub == lane

    def step(k, carry):
        rest, solved = carry
        column = jnp.sum(jnp.where(lane == k, rest, 0.0), axis=1, keepdims=True)
        pivot = jnp.sum(jnp.where(sub_col == k, column, 0.0), axis=0, keepdims=True)
        root = jnp.sqrt(pivot)
        l_col = jnp.where(sub_col >= k, column / root, 0.0)
        l_row = jnp.sum(jnp.where(eye, l_col, 0.0), axis=0, keepdims=True)
        rest = rest - l_col * l_row
        row_k = jnp.sum(jnp.where(sub == k, solved, 0.0), axis=0, keepdims=True) / root
        below = jnp.where(sub_col > k, l_col, 0.0)
        solved = jnp.where(sub == k, row_k, solved - below * row_k)
        upper_ref[pl.ds(k, 1), :] = l_row
        return rest, solved

    start = (gram_ref[...], jnp.where(eye, 1.0, 0.0).astype(jnp.float32))
    _, solved = lax.fori_loop(0, n, step, start)
    lower_inv_ref[...] = solved


def factor(gram):
    n = gram.shape[0]
    vmem = pl.BlockSpec(memory_space=pltpu.VMEM)
    return pl.pallas_call(
        factor_kernel,
        out_shape=(
            jax.ShapeDtypeStruct((n, n), jnp.float32),
            jax.ShapeDtypeStruct((n, n), jnp.float32),
        ),
        in_specs=[vmem],
        out_specs=(vmem, vmem),
        cost_estimate=pl.CostEstimate(
            flops=8 * n * n * n, bytes_accessed=12 * n * n, transcendentals=n
        ),
    )(gram)


IND = ("z", "y")
SNP = ("x", "c")


def shards(genotypes, means, scales, basis_in):
    word_rows, snp_cols = genotypes.shape
    blocks = word_rows // 160
    zeta = lax.map(
        lambda words: standardize(words, means, scales), genotypes.reshape(blocks, 160, snp_cols)
    )
    zeta = zeta.reshape(word_rows * 6, snp_cols)
    local_rows = word_rows * 6
    total_rows = local_rows * lax.axis_size(IND)
    partial_value = lax.dot_general(
        zeta, basis_in, (((0,), (0,)), ((), ())), preferred_element_type=jnp.float32
    )
    loadings = REDUCE_IND(partial_value).astype(jnp.bfloat16)
    sketch_part = jnp.dot(zeta, loadings, preferred_element_type=jnp.float32)
    sketch = REDUCE_SNP(sketch_part)
    gram_local = lax.dot_general(
        sketch, sketch, (((0,), (0,)), ((), ())), precision=lax.Precision.HIGHEST
    )
    gram = REDUCE_IND(gram_local)
    upper, lower_inv = factor(gram)
    factor_n = math.sqrt(total_rows)
    basis = (
        lax.dot_general(
            sketch, lower_inv, (((1,), (1,)), ((), ())), precision=lax.Precision.HIGHEST
        )
        * factor_n
    ).astype(jnp.bfloat16)
    triangle = upper / (total_rows * math.sqrt(SNPS))
    return (basis, triangle)


def butterfly_sum(x, axes):
    for axis in axes:
        size = lax.axis_size(axis)
        distance = 1
        while distance < size:
            pairs = [(i, i ^ distance) for i in range(size)]
            x = x + lax.ppermute(x, axis, pairs)
            distance *= 2
    return x


def REDUCE_IND(x):
    return butterfly_sum(x, ("y", "z"))


def REDUCE_SNP(x):
    return butterfly_sum(x, ("c", "x"))


def solution(mesh):
    ind_size, snp_size = mesh.devices.shape
    grid = Mesh(mesh.devices.reshape(8, ind_size // 8, snp_size // 2, 2), ("z", "y", "x", "c"))
    in_specs = (P(IND, SNP), P(SNP), P(SNP), P(IND, None))
    out_specs = (P(IND, None), P())
    return jax.shard_map(shards, mesh=grid, in_specs=in_specs, out_specs=out_specs, check_vma=False)
```

```python
import math

import jax
import jax.numpy as jnp
from jax import lax
from jax.experimental import pallas as pl
from jax.experimental.pallas import tpu as pltpu
from jax.sharding import Mesh
from jax.sharding import PartitionSpec as P

SNPS = 4096


def standardize(words, means, scales):
    shifts = 2 * jnp.arange(6, dtype=jnp.int32)
    dose = jnp.bitwise_and(jnp.right_shift(words[:, None, :], shifts[None, :, None]), 3)
    values = (dose.astype(jnp.float32) - means) * scales
    return values.astype(jnp.bfloat16).reshape(words.shape[0] * 6, words.shape[1])


def factor_kernel(gram_ref, upper_ref, lower_inv_ref):
    n = gram_ref.shape[0]
    sub = lax.broadcasted_iota(jnp.int32, (n, n), 0)
    lane = lax.broadcasted_iota(jnp.int32, (n, n), 1)
    sub_col = lax.broadcasted_iota(jnp.int32, (n, 1), 0)
    eye = sub == lane

    def step(k, carry):
        rest, solved = carry
        column = jnp.sum(jnp.where(lane == k, rest, 0.0), axis=1, keepdims=True)
        pivot = jnp.sum(jnp.where(sub_col == k, column, 0.0), axis=0, keepdims=True)
        root = jnp.sqrt(pivot)
        l_col = jnp.where(sub_col >= k, column / root, 0.0)
        l_row = jnp.sum(jnp.where(eye, l_col, 0.0), axis=0, keepdims=True)
        rest = rest - l_col * l_row
        row_k = jnp.sum(jnp.where(sub == k, solved, 0.0), axis=0, keepdims=True) / root
        below = jnp.where(sub_col > k, l_col, 0.0)
        solved = jnp.where(sub == k, row_k, solved - below * row_k)
        upper_ref[pl.ds(k, 1), :] = l_row
        return rest, solved

    start = (gram_ref[...], jnp.where(eye, 1.0, 0.0).astype(jnp.float32))
    _, solved = lax.fori_loop(0, n, step, start)
    lower_inv_ref[...] = solved


def factor(gram):
    n = gram.shape[0]
    vmem = pl.BlockSpec(memory_space=pltpu.VMEM)
    return pl.pallas_call(
        factor_kernel,
        out_shape=(
            jax.ShapeDtypeStruct((n, n), jnp.float32),
            jax.ShapeDtypeStruct((n, n), jnp.float32),
        ),
        in_specs=[vmem],
        out_specs=(vmem, vmem),
        cost_estimate=pl.CostEstimate(
            flops=8 * n * n * n, bytes_accessed=12 * n * n, transcendentals=n
        ),
    )(gram)


IND = ("z", "y")
SNP = ("x", "c")


def shards(genotypes, means, scales, basis_in):
    word_rows, snp_cols = genotypes.shape
    blocks = word_rows // 160
    zeta = lax.map(
        lambda words: standardize(words, means, scales), genotypes.reshape(blocks, 160, snp_cols)
    )
    zeta = zeta.reshape(word_rows * 6, snp_cols)
    local_rows = word_rows * 6
    total_rows = local_rows * lax.axis_size(IND)
    partial_value = lax.dot_general(
        zeta, basis_in, (((0,), (0,)), ((), ())), preferred_element_type=jnp.float32
    )
    loadings = REDUCE_IND(partial_value).astype(jnp.bfloat16)
    sketch_part = jnp.dot(zeta, loadings, preferred_element_type=jnp.float32)
    sketch = REDUCE_SNP(sketch_part)
    gram_local = lax.dot_general(
        sketch, sketch, (((0,), (0,)), ((), ())), precision=lax.Precision.HIGHEST
    )
    gram = REDUCE_IND(gram_local)
    upper, lower_inv = factor(gram)
    factor_n = math.sqrt(total_rows)
    basis = (
        lax.dot_general(
            sketch, lower_inv, (((1,), (1,)), ((), ())), precision=lax.Precision.HIGHEST
        )
        * factor_n
    ).astype(jnp.bfloat16)
    triangle = upper / (total_rows * math.sqrt(SNPS))
    return (basis, triangle)


def butterfly_sum(x, axes):
    for axis in axes:
        size = lax.axis_size(axis)
        distance = 1
        while distance < size:
            pairs = [(i, i ^ distance) for i in range(size)]
            x = x + lax.ppermute(x, axis, pairs)
            distance *= 2
    return x


def swap_cores(x):
    return lax.ppermute(x, "c", [(0, 1), (1, 0)])


def REDUCE_IND(x):
    half = x.shape[0] // 2
    first, second = x[:half], x[half:]
    for axis_a, axis_b in (("y", "z"), ("z", "y")):
        first = butterfly_sum(first, (axis_a,))
        second = butterfly_sum(second, (axis_b,))
    return jnp.concatenate([first, second], axis=0)


def REDUCE_SNP(x):
    half = x.shape[0] // 2
    core = lax.axis_index("c")
    top, bottom = x[:half], x[half:]
    mine = jnp.where(core == 0, top, bottom)
    theirs = jnp.where(core == 0, bottom, top)
    mine = mine + swap_cores(theirs)
    mine = butterfly_sum(mine, ("x",))
    other = swap_cores(mine)
    top = jnp.where(core == 0, mine, other)
    bottom = jnp.where(core == 0, other, mine)
    return jnp.concatenate([top, bottom], axis=0)


def solution(mesh):
    ind_size, snp_size = mesh.devices.shape
    grid = Mesh(mesh.devices.reshape(8, ind_size // 8, snp_size // 2, 2), ("z", "y", "x", "c"))
    in_specs = (P(IND, SNP), P(SNP), P(SNP), P(IND, None))
    out_specs = (P(IND, None), P())
    return jax.shard_map(shards, mesh=grid, in_specs=in_specs, out_specs=out_specs, check_vma=False)
```

```python
import math

import jax
import jax.numpy as jnp
from jax import lax
from jax.experimental import pallas as pl
from jax.experimental.pallas import tpu as pltpu
from jax.sharding import Mesh
from jax.sharding import PartitionSpec as P

SNPS = 4096


def standardize(words, means, scales):
    shifts = 2 * jnp.arange(6, dtype=jnp.int32)
    dose = jnp.bitwise_and(jnp.right_shift(words[None, :, :], shifts[:, None, None]), 3)
    values = (dose.astype(jnp.float32) - means) * scales
    return values.astype(jnp.bfloat16).reshape(6 * words.shape[0], words.shape[1])


def factor_kernel(gram_ref, upper_ref, lower_inv_ref):
    n = gram_ref.shape[0]
    sub = lax.broadcasted_iota(jnp.int32, (n, n), 0)
    lane = lax.broadcasted_iota(jnp.int32, (n, n), 1)
    sub_col = lax.broadcasted_iota(jnp.int32, (n, 1), 0)
    eye = sub == lane

    def step(k, carry):
        rest, solved = carry
        column = jnp.sum(jnp.where(lane == k, rest, 0.0), axis=1, keepdims=True)
        pivot = jnp.sum(jnp.where(sub_col == k, column, 0.0), axis=0, keepdims=True)
        root = jnp.sqrt(pivot)
        l_col = jnp.where(sub_col >= k, column / root, 0.0)
        l_row = jnp.sum(jnp.where(eye, l_col, 0.0), axis=0, keepdims=True)
        rest = rest - l_col * l_row
        row_k = jnp.sum(jnp.where(sub == k, solved, 0.0), axis=0, keepdims=True) / root
        below = jnp.where(sub_col > k, l_col, 0.0)
        solved = jnp.where(sub == k, row_k, solved - below * row_k)
        upper_ref[pl.ds(k, 1), :] = l_row
        return rest, solved

    start = (gram_ref[...], jnp.where(eye, 1.0, 0.0).astype(jnp.float32))
    _, solved = lax.fori_loop(0, n, step, start)
    lower_inv_ref[...] = solved


def factor(gram):
    n = gram.shape[0]
    vmem = pl.BlockSpec(memory_space=pltpu.VMEM)
    return pl.pallas_call(
        factor_kernel,
        out_shape=(
            jax.ShapeDtypeStruct((n, n), jnp.float32),
            jax.ShapeDtypeStruct((n, n), jnp.float32),
        ),
        in_specs=[vmem],
        out_specs=(vmem, vmem),
        cost_estimate=pl.CostEstimate(
            flops=8 * n * n * n, bytes_accessed=12 * n * n, transcendentals=n
        ),
    )(gram)


IND = ("z", "y")
SNP = ("x", "c")


def shards(genotypes, means, scales, basis_in):
    word_rows, snp_cols = genotypes.shape
    zeta = standardize(genotypes, means, scales)
    local_rows = word_rows * 6
    total_rows = local_rows * group_size(IND)
    rank = basis_in.shape[1]
    rows_in = basis_in.reshape(word_rows, 6, rank).transpose(1, 0, 2).reshape(local_rows, rank)
    partial_value = lax.dot_general(
        zeta, rows_in, (((0,), (0,)), ((), ())), preferred_element_type=jnp.float32
    )
    loadings = REDUCE_IND(partial_value).astype(jnp.bfloat16)
    sketch_part = jnp.dot(zeta, loadings, preferred_element_type=jnp.float32)
    sketch = REDUCE_SNP(sketch_part)
    gram_local = lax.dot_general(
        sketch, sketch, (((0,), (0,)), ((), ())), precision=lax.Precision.HIGHEST
    )
    gram = REDUCE_IND(gram_local)
    upper, lower_inv = factor(gram)
    factor_n = math.sqrt(total_rows)
    basis = (
        lax.dot_general(
            sketch, lower_inv, (((1,), (1,)), ((), ())), precision=lax.Precision.HIGHEST
        )
        * factor_n
    ).astype(jnp.bfloat16)
    basis = basis.reshape(6, word_rows, rank).transpose(1, 0, 2).reshape(local_rows, rank)
    triangle = upper / (total_rows * math.sqrt(SNPS))
    return (basis, triangle)


def butterfly_sum(x, axes):
    for axis in axes:
        size = lax.axis_size(axis)
        distance = 1
        while distance < size:
            pairs = [(i, i ^ distance) for i in range(size)]
            x = x + lax.ppermute(x, axis, pairs)
            distance *= 2
    return x


def group_size(axes):
    size = 1
    for axis in axes:
        size *= lax.axis_size(axis)
    return size


def reduce_scatter(x, axes):
    size = group_size(axes)
    parts = x.reshape(size, x.shape[0] // size, *x.shape[1:])
    return lax.all_to_all(parts, axes, 0, 0, tiled=False).sum(axis=0)


def all_gather(x, axes):
    size = group_size(axes)
    parts = jnp.broadcast_to(x[None], (size,) + x.shape)
    gathered = lax.all_to_all(parts, axes, 0, 0, tiled=False)
    return gathered.reshape(size * x.shape[0], *x.shape[1:])


def REDUCE_IND(x):
    return all_gather(reduce_scatter(x, IND), IND)


def REDUCE_SNP(x):
    return all_gather(reduce_scatter(x, SNP), SNP)


def solution(mesh):
    ind_size, snp_size = mesh.devices.shape
    grid = Mesh(mesh.devices.reshape(8, ind_size // 8, snp_size // 2, 2), ("z", "y", "x", "c"))
    in_specs = (P(IND, SNP), P(SNP), P(SNP), P(IND, None))
    out_specs = (P(IND, None), P())
    return jax.shard_map(shards, mesh=grid, in_specs=in_specs, out_specs=out_specs, check_vma=False)
```

```python
import functools
import math

import jax
import jax.numpy as jnp
from jax import lax
from jax.experimental import pallas as pl
from jax.experimental.pallas import tpu as pltpu
from jax.sharding import Mesh
from jax.sharding import PartitionSpec as P

SNPS = 4096


def standardize(words, means, scales):
    shifts = 2 * jnp.arange(6, dtype=jnp.int32)
    dose = jnp.bitwise_and(jnp.right_shift(words[None, :, :], shifts[:, None, None]), 3)
    values = (dose.astype(jnp.float32) - means) * scales
    return values.astype(jnp.bfloat16).reshape(6 * words.shape[0], words.shape[1])


def factor_kernel(scale, gram_ref, upper_ref, lower_inv_ref):
    n = gram_ref.shape[0]
    sub = lax.broadcasted_iota(jnp.int32, (n, n), 0)
    lane = lax.broadcasted_iota(jnp.int32, (n, n), 1)
    sub_col = lax.broadcasted_iota(jnp.int32, (n, 1), 0)
    eye = sub == lane

    def step(k, carry):
        rest, solved = carry
        column = jnp.sum(jnp.where(lane == k, rest, 0.0), axis=1, keepdims=True)
        pivot = jnp.sum(jnp.where(sub_col == k, column, 0.0), axis=0, keepdims=True)
        root = jnp.sqrt(pivot)
        l_col = jnp.where(sub_col >= k, column / root, 0.0)
        l_row = jnp.sum(jnp.where(eye, l_col, 0.0), axis=0, keepdims=True)
        rest = rest - l_col * l_row
        row_k = jnp.sum(jnp.where(sub == k, solved, 0.0), axis=0, keepdims=True) / root
        below = jnp.where(sub_col > k, l_col, 0.0)
        solved = jnp.where(sub == k, row_k, solved - below * row_k)
        upper_ref[pl.ds(k, 1), :] = l_row / scale
        return rest, solved

    start = (gram_ref[...], jnp.where(eye, 1.0, 0.0).astype(jnp.float32))
    _, solved = lax.fori_loop(0, n, step, start)
    lower_inv_ref[...] = solved


def factor(gram, scale):
    n = gram.shape[0]
    vmem = pl.BlockSpec(memory_space=pltpu.VMEM)
    return pl.pallas_call(
        functools.partial(factor_kernel, scale),
        out_shape=(
            jax.ShapeDtypeStruct((n, n), jnp.float32),
            jax.ShapeDtypeStruct((n, n), jnp.float32),
        ),
        in_specs=[vmem],
        out_specs=(vmem, vmem),
        cost_estimate=pl.CostEstimate(
            flops=8 * n * n * n, bytes_accessed=12 * n * n, transcendentals=n
        ),
    )(gram)


IND = ("z", "y")
SNP = ("x", "c")


def shards(genotypes, means, scales, basis_in):
    word_rows, snp_cols = genotypes.shape
    zeta = standardize(genotypes, means, scales)
    local_rows = word_rows * 6
    total_rows = local_rows * group_size(IND)
    rank = basis_in.shape[1]
    rows_in = basis_in.reshape(word_rows, 6, rank).transpose(1, 0, 2).reshape(local_rows, rank)
    partial_value = lax.dot_general(
        rows_in, zeta, (((0,), (0,)), ((), ())), preferred_element_type=jnp.float32
    ).T
    loadings = REDUCE_IND(partial_value).astype(jnp.bfloat16)
    sketch_part = jnp.dot(zeta, loadings, preferred_element_type=jnp.float32)
    sketch = REDUCE_SNP(sketch_part)
    gram_local = lax.dot_general(
        sketch, sketch, (((0,), (0,)), ((), ())), precision=lax.Precision.HIGHEST
    )
    gram = REDUCE_IND(gram_local)
    triangle, lower_inv = factor(gram, total_rows * math.sqrt(SNPS))
    factor_n = math.sqrt(total_rows)
    basis = (
        lax.dot_general(
            sketch, lower_inv, (((1,), (1,)), ((), ())), precision=lax.Precision.HIGHEST
        )
        * factor_n
    ).astype(jnp.bfloat16)
    basis = basis.reshape(6, word_rows, rank).transpose(1, 0, 2).reshape(local_rows, rank)
    return (basis, triangle)


def butterfly_sum(x, axes):
    for axis in axes:
        size = lax.axis_size(axis)
        distance = 1
        while distance < size:
            pairs = [(i, i ^ distance) for i in range(size)]
            x = x + lax.ppermute(x, axis, pairs)
            distance *= 2
    return x


def group_size(axes):
    size = 1
    for axis in axes:
        size *= lax.axis_size(axis)
    return size


def reduce_scatter(x, axes):
    size = group_size(axes)
    parts = x.reshape(size, x.shape[0] // size, *x.shape[1:])
    return lax.all_to_all(parts, axes, 0, 0, tiled=False).sum(axis=0)


def all_gather(x, axes):
    size = group_size(axes)
    parts = jnp.broadcast_to(x[None], (size,) + x.shape)
    gathered = lax.all_to_all(parts, axes, 0, 0, tiled=False)
    return gathered.reshape(size * x.shape[0], *x.shape[1:])


def REDUCE_IND(x):
    return all_gather(reduce_scatter(x, IND), IND)


def swap_cores(x):
    return lax.ppermute(x, "c", [(0, 1), (1, 0)])


def REDUCE_SNP(x):
    half = x.shape[0] // 2
    core = lax.axis_index("c")
    top, bottom = x[:half], x[half:]
    mine = jnp.where(core == 0, top, bottom) + swap_cores(jnp.where(core == 0, bottom, top))
    mine = all_gather(reduce_scatter(mine, ("x",)), ("x",))
    other = swap_cores(mine)
    top = jnp.where(core == 0, mine, other)
    bottom = jnp.where(core == 0, other, mine)
    return jnp.concatenate([top, bottom], axis=0)


def solution(mesh):
    ind_size, snp_size = mesh.devices.shape
    grid = Mesh(mesh.devices.reshape(8, ind_size // 8, snp_size // 2, 2), ("z", "y", "x", "c"))
    in_specs = (P(IND, SNP), P(SNP), P(SNP), P(IND, None))
    out_specs = (P(IND, None), P())
    return jax.shard_map(shards, mesh=grid, in_specs=in_specs, out_specs=out_specs, check_vma=False)
```

```python
import functools
import math

import jax
import jax.numpy as jnp
from jax import lax
from jax.experimental import pallas as pl
from jax.experimental.pallas import tpu as pltpu
from jax.sharding import Mesh
from jax.sharding import PartitionSpec as P

SNPS = 4096


def standardize(words, means, scales):
    shifts = 2 * jnp.arange(6, dtype=jnp.int32)
    dose = jnp.bitwise_and(jnp.right_shift(words[None, :, :], shifts[:, None, None]), 3)
    values = (dose.astype(jnp.float32) - means) * scales
    return values.astype(jnp.bfloat16).reshape(6 * words.shape[0], words.shape[1])


def factor_kernel(scale, gram_ref, upper_ref, lower_inv_ref):
    n = gram_ref.shape[0]
    tile = 8
    eye = lax.broadcasted_iota(jnp.int32, (n, n), 0) == lax.broadcasted_iota(jnp.int32, (n, n), 1)
    rest = gram_ref[...]
    solved = jnp.where(eye, 1.0, 0.0).astype(jnp.float32)
    for origin in range(0, n, tile):
        rows = n - origin
        sub = lax.broadcasted_iota(jnp.int32, (rows, n), 0)
        lane = lax.broadcasted_iota(jnp.int32, (rows, n), 1)
        sub_col = lax.broadcasted_iota(jnp.int32, (rows, 1), 0)

        def step(local, carry, origin=origin, sub=sub, lane=lane, sub_col=sub_col):
            rest, solved = carry
            k = origin + local
            column = jnp.sum(jnp.where(lane == k, rest, 0.0), axis=1, keepdims=True)
            pivot = jnp.sum(jnp.where(sub_col == local, column, 0.0), axis=0, keepdims=True)
            root = jnp.sqrt(pivot)
            l_col = jnp.where(sub_col >= local, column / root, 0.0)
            l_row = jnp.sum(jnp.where(lane == sub + origin, l_col, 0.0), axis=0, keepdims=True)
            rest = rest - l_col * l_row
            row_k = jnp.sum(jnp.where(sub == local, solved, 0.0), axis=0, keepdims=True) / root
            below = jnp.where(sub_col > local, l_col, 0.0)
            solved = jnp.where(sub == local, row_k, solved - below * row_k)
            upper_ref[pl.ds(k, 1), :] = l_row / scale
            return rest, solved

        rest, solved = lax.fori_loop(0, tile, step, (rest, solved))
        lower_inv_ref[origin:origin + tile, :] = solved[:tile]
        rest, solved = rest[tile:], solved[tile:]


def factor(gram, scale):
    n = gram.shape[0]
    vmem = pl.BlockSpec(memory_space=pltpu.VMEM)
    return pl.pallas_call(
        functools.partial(factor_kernel, scale),
        out_shape=(
            jax.ShapeDtypeStruct((n, n), jnp.float32),
            jax.ShapeDtypeStruct((n, n), jnp.float32),
        ),
        in_specs=[vmem],
        out_specs=(vmem, vmem),
        cost_estimate=pl.CostEstimate(
            flops=8 * n * n * n, bytes_accessed=12 * n * n, transcendentals=n
        ),
    )(gram)


IND = ("z", "y")
SNP = ("x", "c")


def shards(genotypes, means, scales, basis_in):
    word_rows, snp_cols = genotypes.shape
    zeta = standardize(genotypes, means, scales)
    local_rows = word_rows * 6
    total_rows = local_rows * group_size(IND)
    rank = basis_in.shape[1]
    rows_in = basis_in.reshape(word_rows, 6, rank).transpose(1, 0, 2).reshape(local_rows, rank)
    partial_value = lax.dot_general(
        rows_in, zeta, (((0,), (0,)), ((), ())), preferred_element_type=jnp.float32
    ).T
    loadings = REDUCE_IND(partial_value).astype(jnp.bfloat16)
    sketch_part = jnp.dot(zeta, loadings, preferred_element_type=jnp.float32)
    sketch = REDUCE_SNP(sketch_part)
    gram_local = lax.dot_general(
        sketch, sketch, (((0,), (0,)), ((), ())), precision=lax.Precision.HIGHEST
    )
    gram = REDUCE_IND(gram_local)
    triangle, lower_inv = factor(gram, total_rows * math.sqrt(SNPS))
    factor_n = math.sqrt(total_rows)
    basis = (
        lax.dot_general(
            sketch, lower_inv, (((1,), (1,)), ((), ())), precision=lax.Precision.HIGHEST
        )
        * factor_n
    ).astype(jnp.bfloat16)
    basis = basis.reshape(6, word_rows, rank).transpose(1, 0, 2).reshape(local_rows, rank)
    return (basis, triangle)


def butterfly_sum(x, axes):
    for axis in axes:
        size = lax.axis_size(axis)
        distance = 1
        while distance < size:
            pairs = [(i, i ^ distance) for i in range(size)]
            x = x + lax.ppermute(x, axis, pairs)
            distance *= 2
    return x


def group_size(axes):
    size = 1
    for axis in axes:
        size *= lax.axis_size(axis)
    return size


def reduce_scatter(x, axes):
    size = group_size(axes)
    parts = x.reshape(size, x.shape[0] // size, *x.shape[1:])
    return lax.all_to_all(parts, axes, 0, 0, tiled=False).sum(axis=0)


def all_gather(x, axes):
    size = group_size(axes)
    parts = jnp.broadcast_to(x[None], (size,) + x.shape)
    gathered = lax.all_to_all(parts, axes, 0, 0, tiled=False)
    return gathered.reshape(size * x.shape[0], *x.shape[1:])


def REDUCE_IND(x):
    return all_gather(reduce_scatter(x, IND), IND)


def swap_cores(x):
    return lax.ppermute(x, "c", [(0, 1), (1, 0)])


def REDUCE_SNP(x):
    half = x.shape[0] // 2
    core = lax.axis_index("c")
    top, bottom = x[:half], x[half:]
    mine = jnp.where(core == 0, top, bottom) + swap_cores(jnp.where(core == 0, bottom, top))
    mine = all_gather(reduce_scatter(mine, ("x",)), ("x",))
    other = swap_cores(mine)
    top = jnp.where(core == 0, mine, other)
    bottom = jnp.where(core == 0, other, mine)
    return jnp.concatenate([top, bottom], axis=0)


def solution(mesh):
    ind_size, snp_size = mesh.devices.shape
    grid = Mesh(mesh.devices.reshape(8, ind_size // 8, snp_size // 2, 2), ("z", "y", "x", "c"))
    in_specs = (P(IND, SNP), P(SNP), P(SNP), P(IND, None))
    out_specs = (P(IND, None), P())
    return jax.shard_map(shards, mesh=grid, in_specs=in_specs, out_specs=out_specs, check_vma=False)
```

```python
import functools
import math

import jax
import jax.numpy as jnp
from jax import lax
from jax.experimental import pallas as pl
from jax.experimental.pallas import tpu as pltpu
from jax.sharding import Mesh
from jax.sharding import PartitionSpec as P

SNPS = 4096


def standardize(words, means, scales):
    shifts = 2 * jnp.arange(6, dtype=jnp.int32)
    dose = jnp.bitwise_and(jnp.right_shift(words[None, :, :], shifts[:, None, None]), 3)
    values = (dose.astype(jnp.float32) - means) * scales
    return values.astype(jnp.bfloat16).reshape(6 * words.shape[0], words.shape[1])


def factor_kernel(scale, gram_ref, upper_ref, lower_inv_ref):
    n = gram_ref.shape[0]
    tile = 8
    eye = lax.broadcasted_iota(jnp.int32, (n, n), 0) == lax.broadcasted_iota(jnp.int32, (n, n), 1)
    rest = gram_ref[...]
    solved = jnp.where(eye, 1.0, 0.0).astype(jnp.float32)
    first_lane = lax.broadcasted_iota(jnp.int32, (n, n), 1) == 0
    column = jnp.sum(jnp.where(first_lane, rest, 0.0), axis=1, keepdims=True)
    for origin in range(0, n, tile):
        rows = n - origin
        sub = lax.broadcasted_iota(jnp.int32, (rows, n), 0)
        lane = lax.broadcasted_iota(jnp.int32, (rows, n), 1)
        sub_col = lax.broadcasted_iota(jnp.int32, (rows, 1), 0)

        def step(local, carry, origin=origin, sub=sub, lane=lane, sub_col=sub_col):
            rest, solved, column = carry
            k = origin + local
            pivot = jnp.sum(jnp.where(sub_col == local, column, 0.0), axis=0, keepdims=True)
            root = jnp.sqrt(pivot)
            l_col = jnp.where(sub_col >= local, column / root, 0.0)
            ahead = jnp.sum(jnp.where(lane == k + 1, rest, 0.0), axis=1, keepdims=True)
            l_next = jnp.sum(jnp.where(sub_col == local + 1, l_col, 0.0), axis=0, keepdims=True)
            column = ahead - l_col * l_next
            l_row = jnp.sum(jnp.where(lane == sub + origin, l_col, 0.0), axis=0, keepdims=True)
            rest = rest - l_col * l_row
            row_k = jnp.sum(jnp.where(sub == local, solved, 0.0), axis=0, keepdims=True) / root
            below = jnp.where(sub_col > local, l_col, 0.0)
            solved = jnp.where(sub == local, row_k, solved - below * row_k)
            upper_ref[pl.ds(k, 1), :] = l_row / scale
            return rest, solved, column

        rest, solved, column = lax.fori_loop(0, tile, step, (rest, solved, column))
        lower_inv_ref[origin:origin + tile, :] = solved[:tile]
        rest, solved, column = rest[tile:], solved[tile:], column[tile:]


def factor(gram, scale):
    n = gram.shape[0]
    vmem = pl.BlockSpec(memory_space=pltpu.VMEM)
    return pl.pallas_call(
        functools.partial(factor_kernel, scale),
        out_shape=(
            jax.ShapeDtypeStruct((n, n), jnp.float32),
            jax.ShapeDtypeStruct((n, n), jnp.float32),
        ),
        in_specs=[vmem],
        out_specs=(vmem, vmem),
        cost_estimate=pl.CostEstimate(
            flops=8 * n * n * n, bytes_accessed=12 * n * n, transcendentals=n
        ),
    )(gram)


IND = ("z", "y")
SNP = ("x", "c")


def shards(genotypes, means, scales, basis_in):
    word_rows, snp_cols = genotypes.shape
    zeta = standardize(genotypes, means, scales)
    local_rows = word_rows * 6
    total_rows = local_rows * group_size(IND)
    rank = basis_in.shape[1]
    rows_in = basis_in.reshape(word_rows, 6, rank).transpose(1, 0, 2).reshape(local_rows, rank)
    partial_value = lax.dot_general(
        rows_in, zeta, (((0,), (0,)), ((), ())), preferred_element_type=jnp.float32
    ).T
    loadings = REDUCE_IND(partial_value).astype(jnp.bfloat16)
    sketch_part = jnp.dot(zeta, loadings, preferred_element_type=jnp.float32)
    sketch = REDUCE_SNP(sketch_part)
    gram_local = lax.dot_general(
        sketch, sketch, (((0,), (0,)), ((), ())), precision=lax.Precision.HIGHEST
    )
    gram = REDUCE_IND(gram_local)
    triangle, lower_inv = factor(gram, total_rows * math.sqrt(SNPS))
    factor_n = math.sqrt(total_rows)
    basis = (
        lax.dot_general(
            sketch, lower_inv, (((1,), (1,)), ((), ())), precision=lax.Precision.HIGHEST
        )
        * factor_n
    ).astype(jnp.bfloat16)
    basis = basis.reshape(6, word_rows, rank).transpose(1, 0, 2).reshape(local_rows, rank)
    return (basis, triangle)


def butterfly_sum(x, axes):
    for axis in axes:
        size = lax.axis_size(axis)
        distance = 1
        while distance < size:
            pairs = [(i, i ^ distance) for i in range(size)]
            x = x + lax.ppermute(x, axis, pairs)
            distance *= 2
    return x


def group_size(axes):
    size = 1
    for axis in axes:
        size *= lax.axis_size(axis)
    return size


def reduce_scatter(x, axes):
    size = group_size(axes)
    parts = x.reshape(size, x.shape[0] // size, *x.shape[1:])
    return lax.all_to_all(parts, axes, 0, 0, tiled=False).sum(axis=0)


def all_gather(x, axes):
    size = group_size(axes)
    parts = jnp.broadcast_to(x[None], (size,) + x.shape)
    gathered = lax.all_to_all(parts, axes, 0, 0, tiled=False)
    return gathered.reshape(size * x.shape[0], *x.shape[1:])


def REDUCE_IND(x):
    return all_gather(reduce_scatter(x, IND), IND)


def swap_cores(x):
    return lax.ppermute(x, "c", [(0, 1), (1, 0)])


def REDUCE_SNP(x):
    half = x.shape[0] // 2
    core = lax.axis_index("c")
    top, bottom = x[:half], x[half:]
    mine = jnp.where(core == 0, top, bottom) + swap_cores(jnp.where(core == 0, bottom, top))
    mine = all_gather(reduce_scatter(mine, ("x",)), ("x",))
    other = swap_cores(mine)
    top = jnp.where(core == 0, mine, other)
    bottom = jnp.where(core == 0, other, mine)
    return jnp.concatenate([top, bottom], axis=0)


def solution(mesh):
    ind_size, snp_size = mesh.devices.shape
    grid = Mesh(mesh.devices.reshape(8, ind_size // 8, snp_size // 2, 2), ("z", "y", "x", "c"))
    in_specs = (P(IND, SNP), P(SNP), P(SNP), P(IND, None))
    out_specs = (P(IND, None), P())
    return jax.shard_map(shards, mesh=grid, in_specs=in_specs, out_specs=out_specs, check_vma=False)
```

```python
import functools
import math

import jax
import jax.numpy as jnp
from jax import lax
from jax.experimental import pallas as pl
from jax.experimental.pallas import tpu as pltpu
from jax.sharding import Mesh
from jax.sharding import PartitionSpec as P

SNPS = 4096


def standardize(words, means, scales):
    shifts = 2 * jnp.arange(6, dtype=jnp.int32)
    dose = jnp.bitwise_and(jnp.right_shift(words[None, :, :], shifts[:, None, None]), 3)
    values = (dose.astype(jnp.float32) - means) * scales
    return values.astype(jnp.bfloat16).reshape(6 * words.shape[0], words.shape[1])


def factor_kernel(scale, gram_ref, upper_ref, lower_inv_ref):
    n = gram_ref.shape[0]
    tile = 8
    sub_full = lax.broadcasted_iota(jnp.int32, (n, n), 0)
    lane_full = lax.broadcasted_iota(jnp.int32, (n, n), 1)
    rest = gram_ref[...]
    solved = jnp.where(sub_full == lane_full, 1.0, 0.0).astype(jnp.float32)
    column = jnp.sum(jnp.where(lane_full == 0, rest, 0.0), axis=1, keepdims=True)
    pivot = jnp.sum(jnp.where((lane_full == 0) & (sub_full == 0), rest, 0.0), keepdims=True)
    row_pre = solved[0:1, :]
    for origin in range(0, n, tile):
        rows = n - origin
        sub = lax.broadcasted_iota(jnp.int32, (rows, n), 0)
        lane = lax.broadcasted_iota(jnp.int32, (rows, n), 1)
        sub_col = lax.broadcasted_iota(jnp.int32, (rows, 1), 0)

        def step(local, carry, origin=origin, sub=sub, lane=lane, sub_col=sub_col):
            rest, solved, column, pivot, row_pre = carry
            k = origin + local
            root = jnp.sqrt(pivot)
            ahead = jnp.sum(jnp.where(lane == k + 1, rest, 0.0), axis=1, keepdims=True)
            ahead_pivot = jnp.sum(jnp.where(sub_col == local + 1, ahead, 0.0), axis=0, keepdims=True)
            column_next = jnp.sum(jnp.where(sub_col == local + 1, column, 0.0), axis=0, keepdims=True)
            ahead_row = jnp.sum(jnp.where(sub == local + 1, solved, 0.0), axis=0, keepdims=True)
            l_col = jnp.where(sub_col >= local, column / root, 0.0)
            l_next = column_next / root
            row_k = row_pre / root
            pivot = ahead_pivot - l_next * l_next
            column = ahead - l_col * l_next
            row_pre = ahead_row - l_next * row_k
            l_row = jnp.sum(jnp.where(lane == sub + origin, l_col, 0.0), axis=0, keepdims=True)
            rest = rest - l_col * l_row
            below = jnp.where(sub_col > local, l_col, 0.0)
            solved = jnp.where(sub == local, row_k, solved - below * row_k)
            upper_ref[pl.ds(k, 1), :] = l_row / scale
            return rest, solved, column, pivot, row_pre

        carry = (rest, solved, column, pivot, row_pre)
        rest, solved, column, pivot, row_pre = lax.fori_loop(0, tile, step, carry, unroll=True)
        lower_inv_ref[origin:origin + tile, :] = solved[:tile]
        rest, solved, column = rest[tile:], solved[tile:], column[tile:]


def factor(gram, scale):
    n = gram.shape[0]
    vmem = pl.BlockSpec(memory_space=pltpu.VMEM)
    return pl.pallas_call(
        functools.partial(factor_kernel, scale),
        out_shape=(
            jax.ShapeDtypeStruct((n, n), jnp.float32),
            jax.ShapeDtypeStruct((n, n), jnp.float32),
        ),
        in_specs=[vmem],
        out_specs=(vmem, vmem),
        cost_estimate=pl.CostEstimate(
            flops=8 * n * n * n, bytes_accessed=12 * n * n, transcendentals=n
        ),
    )(gram)


IND = ("z", "y")
SNP = ("x", "c")


def shards(genotypes, means, scales, basis_in):
    word_rows, snp_cols = genotypes.shape
    zeta = standardize(genotypes, means, scales)
    local_rows = word_rows * 6
    total_rows = local_rows * group_size(IND)
    rank = basis_in.shape[1]
    rows_in = basis_in.reshape(word_rows, 6, rank).transpose(1, 0, 2).reshape(local_rows, rank)
    partial_value = lax.dot_general(
        rows_in, zeta, (((0,), (0,)), ((), ())), preferred_element_type=jnp.float32
    ).T
    loadings = REDUCE_IND(partial_value).astype(jnp.bfloat16)
    sketch_part = jnp.dot(zeta, loadings, preferred_element_type=jnp.float32)
    sketch = REDUCE_SNP(sketch_part)
    gram_local = lax.dot_general(
        sketch, sketch, (((0,), (0,)), ((), ())), precision=lax.Precision.HIGHEST
    )
    gram = REDUCE_IND(gram_local)
    triangle, lower_inv = factor(gram, total_rows * math.sqrt(SNPS))
    factor_n = math.sqrt(total_rows)
    basis = (
        lax.dot_general(
            sketch, lower_inv, (((1,), (1,)), ((), ())), precision=lax.Precision.HIGHEST
        )
        * factor_n
    ).astype(jnp.bfloat16)
    basis = basis.reshape(6, word_rows, rank).transpose(1, 0, 2).reshape(local_rows, rank)
    return (basis, triangle)


def butterfly_sum(x, axes):
    for axis in axes:
        size = lax.axis_size(axis)
        distance = 1
        while distance < size:
            pairs = [(i, i ^ distance) for i in range(size)]
            x = x + lax.ppermute(x, axis, pairs)
            distance *= 2
    return x


def group_size(axes):
    size = 1
    for axis in axes:
        size *= lax.axis_size(axis)
    return size


def reduce_scatter(x, axes):
    size = group_size(axes)
    parts = x.reshape(size, x.shape[0] // size, *x.shape[1:])
    return lax.all_to_all(parts, axes, 0, 0, tiled=False).sum(axis=0)


def all_gather(x, axes):
    size = group_size(axes)
    parts = jnp.broadcast_to(x[None], (size,) + x.shape)
    gathered = lax.all_to_all(parts, axes, 0, 0, tiled=False)
    return gathered.reshape(size * x.shape[0], *x.shape[1:])


def REDUCE_IND(x):
    return all_gather(reduce_scatter(x, IND), IND)


def swap_cores(x):
    return lax.ppermute(x, "c", [(0, 1), (1, 0)])


def REDUCE_SNP(x):
    half = x.shape[0] // 2
    core = lax.axis_index("c")
    top, bottom = x[:half], x[half:]
    mine = jnp.where(core == 0, top, bottom) + swap_cores(jnp.where(core == 0, bottom, top))
    mine = all_gather(reduce_scatter(mine, ("x",)), ("x",))
    other = swap_cores(mine)
    top = jnp.where(core == 0, mine, other)
    bottom = jnp.where(core == 0, other, mine)
    return jnp.concatenate([top, bottom], axis=0)


def solution(mesh):
    ind_size, snp_size = mesh.devices.shape
    grid = Mesh(mesh.devices.reshape(8, ind_size // 8, snp_size // 2, 2), ("z", "y", "x", "c"))
    in_specs = (P(IND, SNP), P(SNP), P(SNP), P(IND, None))
    out_specs = (P(IND, None), P())
    return jax.shard_map(shards, mesh=grid, in_specs=in_specs, out_specs=out_specs, check_vma=False)
```

```python
import functools
import math

import jax
import jax.numpy as jnp
from jax import lax
from jax.experimental import pallas as pl
from jax.experimental.pallas import tpu as pltpu
from jax.sharding import Mesh
from jax.sharding import PartitionSpec as P

SNPS = 4096


def standardize(words, means, scales):
    shifts = 2 * jnp.arange(6, dtype=jnp.int32)
    dose = jnp.bitwise_and(jnp.right_shift(words[None, :, :], shifts[:, None, None]), 3)
    values = (dose.astype(jnp.float32) - means) * scales
    return values.astype(jnp.bfloat16).reshape(6 * words.shape[0], words.shape[1])


def factor_kernel(scale, gram_ref, upper_ref, lower_inv_ref):
    n = gram_ref.shape[0]
    tile = 8
    sub_full = lax.broadcasted_iota(jnp.int32, (n, n), 0)
    lane_full = lax.broadcasted_iota(jnp.int32, (n, n), 1)
    rest = gram_ref[...]
    solved = jnp.where(sub_full == lane_full, 1.0, 0.0).astype(jnp.float32)
    column = jnp.sum(jnp.where(lane_full == 0, rest, 0.0), axis=1, keepdims=True)
    pivot = jnp.sum(jnp.where((lane_full == 0) & (sub_full == 0), rest, 0.0), keepdims=True)
    row_pre = solved[0:1, :]
    for origin in range(0, n, tile):
        rows = n - origin
        sub = lax.broadcasted_iota(jnp.int32, (rows, n), 0)
        lane = lax.broadcasted_iota(jnp.int32, (rows, n), 1)
        sub_col = lax.broadcasted_iota(jnp.int32, (rows, 1), 0)

        def step(local, carry, origin=origin, sub=sub, lane=lane, sub_col=sub_col):
            rest, solved, column, pivot, row_pre = carry
            k = origin + local
            root = jnp.sqrt(pivot)
            ahead = jnp.sum(jnp.where(lane == k + 1, rest, 0.0), axis=1, keepdims=True)
            ahead_pivot = jnp.sum(jnp.where(sub_col == local + 1, ahead, 0.0), axis=0, keepdims=True)
            column_next = jnp.sum(jnp.where(sub_col == local + 1, column, 0.0), axis=0, keepdims=True)
            ahead_row = jnp.sum(jnp.where(sub == local + 1, solved, 0.0), axis=0, keepdims=True)
            l_col = jnp.where(sub_col >= local, column / root, 0.0)
            l_next = column_next / root
            row_k = row_pre / root
            pivot = ahead_pivot - l_next * l_next
            column = ahead - l_col * l_next
            row_pre = ahead_row - l_next * row_k
            l_row = jnp.sum(jnp.where(lane == sub + origin, l_col, 0.0), axis=0, keepdims=True)
            rest = rest - l_col * l_row
            below = jnp.where(sub_col > local, l_col, 0.0)
            solved = jnp.where(sub == local, row_k, solved - below * row_k)
            upper_ref[pl.ds(k, 1), :] = l_row / scale
            return rest, solved, column, pivot, row_pre

        carry = (rest, solved, column, pivot, row_pre)
        rest, solved, column, pivot, row_pre = lax.fori_loop(0, tile, step, carry, unroll=True)
        lower_inv_ref[origin:origin + tile, :] = solved[:tile]
        rest, solved, column = rest[tile:], solved[tile:], column[tile:]


def factor(gram, scale):
    n = gram.shape[0]
    vmem = pl.BlockSpec(memory_space=pltpu.VMEM)
    return pl.pallas_call(
        functools.partial(factor_kernel, scale),
        out_shape=(
            jax.ShapeDtypeStruct((n, n), jnp.float32),
            jax.ShapeDtypeStruct((n, n), jnp.float32),
        ),
        in_specs=[vmem],
        out_specs=(vmem, vmem),
        cost_estimate=pl.CostEstimate(
            flops=8 * n * n * n, bytes_accessed=12 * n * n, transcendentals=n
        ),
    )(gram)


IND = ("z", "y")
SNP = ("x", "c")


def shards(genotypes, means, scales, basis_in):
    word_rows, snp_cols = genotypes.shape
    zeta = standardize(genotypes, means, scales)
    local_rows = word_rows * 6
    total_rows = local_rows * group_size(IND)
    rank = basis_in.shape[1]
    rows_in = basis_in.reshape(word_rows, 6, rank).transpose(1, 0, 2).reshape(local_rows, rank)
    partial_value = lax.dot_general(
        rows_in, zeta, (((0,), (0,)), ((), ())), preferred_element_type=jnp.float32
    ).T
    loadings = REDUCE_IND(partial_value).astype(jnp.bfloat16)
    sketch_part = jnp.dot(zeta, loadings, preferred_element_type=jnp.float32)
    half = local_rows // 2
    core = lax.axis_index("c")
    top, bottom = sketch_part[:half], sketch_part[half:]
    mine = jnp.where(core == 0, top, bottom) + swap_cores(jnp.where(core == 0, bottom, top))
    mine = all_gather(reduce_scatter(mine, ("x",)), ("x",))
    other = swap_cores(mine)
    gram_local = lax.dot_general(
        mine, mine, (((0,), (0,)), ((), ())), precision=lax.Precision.HIGHEST
    )
    gram = all_gather(reduce_scatter(gram_local, IND + ("c",)), IND + ("c",))
    sketch = jnp.concatenate(
        [jnp.where(core == 0, mine, other), jnp.where(core == 0, other, mine)], axis=0
    )
    triangle, lower_inv = factor(gram, total_rows * math.sqrt(SNPS))
    factor_n = math.sqrt(total_rows)
    basis = (
        lax.dot_general(
            sketch, lower_inv, (((1,), (1,)), ((), ())), precision=lax.Precision.HIGHEST
        )
        * factor_n
    ).astype(jnp.bfloat16)
    basis = basis.reshape(6, word_rows, rank).transpose(1, 0, 2).reshape(local_rows, rank)
    return (basis, triangle)


def butterfly_sum(x, axes):
    for axis in axes:
        size = lax.axis_size(axis)
        distance = 1
        while distance < size:
            pairs = [(i, i ^ distance) for i in range(size)]
            x = x + lax.ppermute(x, axis, pairs)
            distance *= 2
    return x


def group_size(axes):
    size = 1
    for axis in axes:
        size *= lax.axis_size(axis)
    return size


def reduce_scatter(x, axes):
    size = group_size(axes)
    parts = x.reshape(size, x.shape[0] // size, *x.shape[1:])
    return lax.all_to_all(parts, axes, 0, 0, tiled=False).sum(axis=0)


def all_gather(x, axes):
    size = group_size(axes)
    parts = jnp.broadcast_to(x[None], (size,) + x.shape)
    gathered = lax.all_to_all(parts, axes, 0, 0, tiled=False)
    return gathered.reshape(size * x.shape[0], *x.shape[1:])


def REDUCE_IND(x):
    return all_gather(reduce_scatter(x, IND), IND)


def swap_cores(x):
    return lax.ppermute(x, "c", [(0, 1), (1, 0)])


def solution(mesh):
    ind_size, snp_size = mesh.devices.shape
    grid = Mesh(mesh.devices.reshape(8, ind_size // 8, snp_size // 2, 2), ("z", "y", "x", "c"))
    in_specs = (P(IND, SNP), P(SNP), P(SNP), P(IND, None))
    out_specs = (P(IND, None), P())
    return jax.shard_map(shards, mesh=grid, in_specs=in_specs, out_specs=out_specs, check_vma=False)
```

```python
import functools
import math

import jax
import jax.numpy as jnp
from jax import lax
from jax.experimental import pallas as pl
from jax.experimental.pallas import tpu as pltpu
from jax.sharding import Mesh
from jax.sharding import PartitionSpec as P

SNPS = 4096


def standardize(words, means, scales):
    shifts = 2 * jnp.arange(6, dtype=jnp.int32)
    dose = jnp.bitwise_and(jnp.right_shift(words[None, :, :], shifts[:, None, None]), 3)
    values = (dose.astype(jnp.float32) - means) * scales
    return values.astype(jnp.bfloat16).reshape(6 * words.shape[0], words.shape[1])


def factor_kernel(scale, gram_ref, upper_ref, lower_inv_ref):
    n = gram_ref.shape[0]
    tile = 8
    sub_full = lax.broadcasted_iota(jnp.int32, (n, n), 0)
    lane_full = lax.broadcasted_iota(jnp.int32, (n, n), 1)
    rest = gram_ref[...]
    solved = jnp.where(sub_full == lane_full, 1.0, 0.0).astype(jnp.float32)
    column = jnp.sum(jnp.where(lane_full == 0, rest, 0.0), axis=1, keepdims=True)
    pivot = jnp.sum(jnp.where((lane_full == 0) & (sub_full == 0), rest, 0.0), keepdims=True)
    row_pre = solved[0:1, :]
    for origin in range(0, n, tile):
        rows = n - origin
        sub = lax.broadcasted_iota(jnp.int32, (rows, n), 0)
        lane = lax.broadcasted_iota(jnp.int32, (rows, n), 1)
        sub_col = lax.broadcasted_iota(jnp.int32, (rows, 1), 0)

        def step(local, carry, origin=origin, sub=sub, lane=lane, sub_col=sub_col):
            rest, solved, column, pivot, row_pre = carry
            k = origin + local
            root = jnp.sqrt(pivot)
            ahead = jnp.sum(jnp.where(lane == k + 1, rest, 0.0), axis=1, keepdims=True)
            ahead_pivot = jnp.sum(jnp.where(sub_col == local + 1, ahead, 0.0), axis=0, keepdims=True)
            column_next = jnp.sum(jnp.where(sub_col == local + 1, column, 0.0), axis=0, keepdims=True)
            ahead_row = jnp.sum(jnp.where(sub == local + 1, solved, 0.0), axis=0, keepdims=True)
            l_col = jnp.where(sub_col >= local, column / root, 0.0)
            l_next = column_next / root
            row_k = row_pre / root
            pivot = ahead_pivot - l_next * l_next
            column = ahead - l_col * l_next
            row_pre = ahead_row - l_next * row_k
            l_row = jnp.sum(jnp.where(lane == sub + origin, l_col, 0.0), axis=0, keepdims=True)
            rest = rest - l_col * l_row
            solved = solved - jnp.where(sub_col > local, l_col, 0.0) * row_k
            upper_ref[pl.ds(k, 1), :] = l_row / scale
            lower_inv_ref[pl.ds(k, 1), :] = row_k
            return rest, solved, column, pivot, row_pre

        carry = (rest, solved, column, pivot, row_pre)
        rest, solved, column, pivot, row_pre = lax.fori_loop(0, tile, step, carry, unroll=True)
        rest, solved, column = rest[tile:], solved[tile:], column[tile:]


def factor(gram, scale):
    n = gram.shape[0]
    vmem = pl.BlockSpec(memory_space=pltpu.VMEM)
    return pl.pallas_call(
        functools.partial(factor_kernel, scale),
        out_shape=(
            jax.ShapeDtypeStruct((n, n), jnp.float32),
            jax.ShapeDtypeStruct((n, n), jnp.float32),
        ),
        in_specs=[vmem],
        out_specs=(vmem, vmem),
        cost_estimate=pl.CostEstimate(
            flops=8 * n * n * n, bytes_accessed=12 * n * n, transcendentals=n
        ),
    )(gram)


IND = ("z", "y")
SNP = ("x", "c")


def shards(genotypes, means, scales, basis_in):
    word_rows, snp_cols = genotypes.shape
    zeta = standardize(genotypes, means, scales)
    local_rows = word_rows * 6
    total_rows = local_rows * group_size(IND)
    rank = basis_in.shape[1]
    rows_in = basis_in.reshape(word_rows, 6, rank).transpose(1, 0, 2).reshape(local_rows, rank)
    partial_value = lax.dot_general(
        rows_in, zeta, (((0,), (0,)), ((), ())), preferred_element_type=jnp.float32
    ).T
    loadings = REDUCE_IND(partial_value).astype(jnp.bfloat16)
    sketch_part = jnp.dot(zeta, loadings, preferred_element_type=jnp.float32)
    half = local_rows // 2
    core = lax.axis_index("c")
    top, bottom = sketch_part[:half], sketch_part[half:]
    mine = jnp.where(core == 0, top, bottom) + swap_cores(jnp.where(core == 0, bottom, top))
    mine = all_gather(reduce_scatter(mine, ("x",)), ("x",))
    other = swap_cores(mine)
    gram_local = lax.dot_general(
        mine, mine, (((0,), (0,)), ((), ())), precision=lax.Precision.HIGHEST
    )
    gram = all_gather(reduce_scatter(gram_local, IND + ("c",)), IND + ("c",))
    sketch = jnp.concatenate(
        [jnp.where(core == 0, mine, other), jnp.where(core == 0, other, mine)], axis=0
    )
    triangle, lower_inv = factor(gram, total_rows * math.sqrt(SNPS))
    factor_n = math.sqrt(total_rows)
    basis = (
        lax.dot_general(
            sketch, lower_inv, (((1,), (1,)), ((), ())), precision=lax.Precision.HIGHEST
        )
        * factor_n
    ).astype(jnp.bfloat16)
    basis = basis.reshape(6, word_rows, rank).transpose(1, 0, 2).reshape(local_rows, rank)
    return (basis, triangle)


def butterfly_sum(x, axes):
    for axis in axes:
        size = lax.axis_size(axis)
        distance = 1
        while distance < size:
            pairs = [(i, i ^ distance) for i in range(size)]
            x = x + lax.ppermute(x, axis, pairs)
            distance *= 2
    return x


def group_size(axes):
    size = 1
    for axis in axes:
        size *= lax.axis_size(axis)
    return size


def reduce_scatter(x, axes):
    size = group_size(axes)
    parts = x.reshape(size, x.shape[0] // size, *x.shape[1:])
    return lax.all_to_all(parts, axes, 0, 0, tiled=False).sum(axis=0)


def all_gather(x, axes):
    size = group_size(axes)
    parts = jnp.broadcast_to(x[None], (size,) + x.shape)
    gathered = lax.all_to_all(parts, axes, 0, 0, tiled=False)
    return gathered.reshape(size * x.shape[0], *x.shape[1:])


def REDUCE_IND(x):
    return all_gather(reduce_scatter(x, IND), IND)


def swap_cores(x):
    return lax.ppermute(x, "c", [(0, 1), (1, 0)])


def solution(mesh):
    ind_size, snp_size = mesh.devices.shape
    grid = Mesh(mesh.devices.reshape(8, ind_size // 8, snp_size // 2, 2), ("z", "y", "x", "c"))
    in_specs = (P(IND, SNP), P(SNP), P(SNP), P(IND, None))
    out_specs = (P(IND, None), P())
    return jax.shard_map(shards, mesh=grid, in_specs=in_specs, out_specs=out_specs, check_vma=False)
```

```python
import functools
import math

import jax
import jax.numpy as jnp
from jax import lax
from jax.experimental import pallas as pl
from jax.experimental.pallas import tpu as pltpu
from jax.sharding import Mesh
from jax.sharding import PartitionSpec as P

SNPS = 4096


def standardize(words, means, scales):
    shifts = 2 * jnp.arange(6, dtype=jnp.int32)
    dose = jnp.bitwise_and(jnp.right_shift(words[None, :, :], shifts[:, None, None]), 3)
    values = (dose.astype(jnp.float32) - means) * scales
    return values.astype(jnp.bfloat16).reshape(6 * words.shape[0], words.shape[1])


def factor_kernel(scale, gram_ref, upper_ref, lower_inv_ref):
    n = gram_ref.shape[0]
    tile = 8
    sub_full = lax.broadcasted_iota(jnp.int32, (n, n), 0)
    lane_full = lax.broadcasted_iota(jnp.int32, (n, n), 1)
    rest = gram_ref[...]
    solved = jnp.where(sub_full == lane_full, 1.0, 0.0).astype(jnp.float32)
    column = jnp.sum(jnp.where(lane_full == 0, rest, 0.0), axis=1, keepdims=True)
    pivot = jnp.sum(jnp.where((lane_full == 0) & (sub_full == 0), rest, 0.0), keepdims=True)
    row_pre = solved[0:1, :]
    for origin in range(0, n, tile):
        rows = n - origin
        sub = lax.broadcasted_iota(jnp.int32, (rows, n), 0)
        lane = lax.broadcasted_iota(jnp.int32, (rows, n), 1)
        sub_col = lax.broadcasted_iota(jnp.int32, (rows, 1), 0)

        def step(local, carry, origin=origin, sub=sub, lane=lane, sub_col=sub_col):
            rest, solved, column, pivot, row_pre = carry
            k = origin + local
            root = jnp.sqrt(pivot)
            ahead = jnp.sum(jnp.where(lane == k + 1, rest, 0.0), axis=1, keepdims=True)
            ahead_pivot = jnp.sum(jnp.where(sub_col == local + 1, ahead, 0.0), axis=0, keepdims=True)
            column_next = jnp.sum(jnp.where(sub_col == local + 1, column, 0.0), axis=0, keepdims=True)
            ahead_row = jnp.sum(jnp.where(sub == local + 1, solved, 0.0), axis=0, keepdims=True)
            l_col = jnp.where(sub_col >= local, column / root, 0.0)
            l_next = column_next / root
            row_k = row_pre / root
            pivot = ahead_pivot - l_next * l_next
            column = ahead - l_col * l_next
            row_pre = ahead_row - l_next * row_k
            l_row = jnp.sum(jnp.where(lane == sub + origin, l_col, 0.0), axis=0, keepdims=True)
            rest = rest - l_col * l_row
            solved = solved - jnp.where(sub_col > local, l_col, 0.0) * row_k
            upper_ref[pl.ds(k, 1), :] = l_row / scale
            lower_inv_ref[pl.ds(k, 1), :] = row_k
            return rest, solved, column, pivot, row_pre

        carry = (rest, solved, column, pivot, row_pre)
        rest, solved, column, pivot, row_pre = lax.fori_loop(0, tile, step, carry, unroll=True)
        rest, solved, column = rest[tile:], solved[tile:], column[tile:]


def factor(gram, scale):
    n = gram.shape[0]
    vmem = pl.BlockSpec(memory_space=pltpu.VMEM)
    return pl.pallas_call(
        functools.partial(factor_kernel, scale),
        out_shape=(
            jax.ShapeDtypeStruct((n, n), jnp.float32),
            jax.ShapeDtypeStruct((n, n), jnp.float32),
        ),
        in_specs=[vmem],
        out_specs=(vmem, vmem),
        cost_estimate=pl.CostEstimate(
            flops=8 * n * n * n, bytes_accessed=12 * n * n, transcendentals=n
        ),
    )(gram)


IND = ("z", "y")
SNP = ("x", "c")


def shards(genotypes, means, scales, basis_in):
    word_rows, snp_cols = genotypes.shape
    zeta = lax.optimization_barrier(standardize(genotypes, means, scales))
    local_rows = word_rows * 6
    total_rows = local_rows * group_size(IND)
    rank = basis_in.shape[1]
    rows_in = basis_in.reshape(word_rows, 6, rank).transpose(1, 0, 2).reshape(local_rows, rank)
    partial_value = lax.dot_general(
        rows_in, zeta, (((0,), (0,)), ((), ())), preferred_element_type=jnp.float32
    ).T
    loadings = REDUCE_IND(partial_value).astype(jnp.bfloat16)
    sketch_part = jnp.dot(zeta, loadings, preferred_element_type=jnp.float32)
    half = local_rows // 2
    core = lax.axis_index("c")
    top, bottom = sketch_part[:half], sketch_part[half:]
    mine = jnp.where(core == 0, top, bottom) + swap_cores(jnp.where(core == 0, bottom, top))
    mine = all_gather(reduce_scatter(mine, ("x",)), ("x",))
    other = swap_cores(mine)
    gram_local = lax.dot_general(
        mine, mine, (((0,), (0,)), ((), ())), precision=lax.Precision.HIGHEST
    )
    gram = all_gather(reduce_scatter(gram_local, IND + ("c",)), IND + ("c",))
    sketch = jnp.concatenate(
        [jnp.where(core == 0, mine, other), jnp.where(core == 0, other, mine)], axis=0
    )
    triangle, lower_inv = factor(gram, total_rows * math.sqrt(SNPS))
    factor_n = math.sqrt(total_rows)
    basis = (
        lax.dot_general(
            sketch, lower_inv, (((1,), (1,)), ((), ())), precision=lax.Precision.HIGHEST
        )
        * factor_n
    ).astype(jnp.bfloat16)
    basis = basis.reshape(6, word_rows, rank).transpose(1, 0, 2).reshape(local_rows, rank)
    return (basis, triangle)


def butterfly_sum(x, axes):
    for axis in axes:
        size = lax.axis_size(axis)
        distance = 1
        while distance < size:
            pairs = [(i, i ^ distance) for i in range(size)]
            x = x + lax.ppermute(x, axis, pairs)
            distance *= 2
    return x


def group_size(axes):
    size = 1
    for axis in axes:
        size *= lax.axis_size(axis)
    return size


def reduce_scatter(x, axes):
    size = group_size(axes)
    parts = x.reshape(size, x.shape[0] // size, *x.shape[1:])
    return lax.all_to_all(parts, axes, 0, 0, tiled=False).sum(axis=0)


def all_gather(x, axes):
    size = group_size(axes)
    parts = jnp.broadcast_to(x[None], (size,) + x.shape)
    gathered = lax.all_to_all(parts, axes, 0, 0, tiled=False)
    return gathered.reshape(size * x.shape[0], *x.shape[1:])


def REDUCE_IND(x):
    return all_gather(reduce_scatter(x, IND), IND)


def swap_cores(x):
    return lax.ppermute(x, "c", [(0, 1), (1, 0)])


def solution(mesh):
    ind_size, snp_size = mesh.devices.shape
    grid = Mesh(mesh.devices.reshape(8, ind_size // 8, snp_size // 2, 2), ("z", "y", "x", "c"))
    in_specs = (P(IND, SNP), P(SNP), P(SNP), P(IND, None))
    out_specs = (P(IND, None), P())
    return jax.shard_map(shards, mesh=grid, in_specs=in_specs, out_specs=out_specs, check_vma=False)
```

```python
import functools
import math

import jax
import jax.numpy as jnp
from jax import lax
from jax.experimental import pallas as pl
from jax.experimental.pallas import tpu as pltpu
from jax.sharding import Mesh
from jax.sharding import PartitionSpec as P

SNPS = 4096


def standardize(words, means, scales):
    shifts = 2 * jnp.arange(6, dtype=jnp.int32)
    dose = jnp.bitwise_and(jnp.right_shift(words[None, :, :], shifts[:, None, None]), 3)
    values = (dose.astype(jnp.float32) - means) * scales
    return values.astype(jnp.bfloat16).reshape(6 * words.shape[0], words.shape[1])


def factor_kernel(scale, gain, gram_ref, sketch_ref, upper_ref, basis_ref, lower_inv_ref):
    n = gram_ref.shape[0]
    tile = 8
    sub_full = lax.broadcasted_iota(jnp.int32, (n, n), 0)
    lane_full = lax.broadcasted_iota(jnp.int32, (n, n), 1)
    rest = gram_ref[...]
    solved = jnp.where(sub_full == lane_full, 1.0, 0.0).astype(jnp.float32)
    column = jnp.sum(jnp.where(lane_full == 0, rest, 0.0), axis=1, keepdims=True)
    pivot = jnp.sum(jnp.where((lane_full == 0) & (sub_full == 0), rest, 0.0), keepdims=True)
    row_pre = solved[0:1, :]
    for origin in range(0, n, tile):
        rows = n - origin
        sub = lax.broadcasted_iota(jnp.int32, (rows, n), 0)
        lane = lax.broadcasted_iota(jnp.int32, (rows, n), 1)
        sub_col = lax.broadcasted_iota(jnp.int32, (rows, 1), 0)

        def step(local, carry, origin=origin, sub=sub, lane=lane, sub_col=sub_col):
            rest, solved, column, pivot, row_pre = carry
            k = origin + local
            root = jnp.sqrt(pivot)
            ahead = jnp.sum(jnp.where(lane == k + 1, rest, 0.0), axis=1, keepdims=True)
            ahead_pivot = jnp.sum(jnp.where(sub_col == local + 1, ahead, 0.0), axis=0, keepdims=True)
            column_next = jnp.sum(jnp.where(sub_col == local + 1, column, 0.0), axis=0, keepdims=True)
            ahead_row = jnp.sum(jnp.where(sub == local + 1, solved, 0.0), axis=0, keepdims=True)
            l_col = jnp.where(sub_col >= local, column / root, 0.0)
            l_next = column_next / root
            row_k = row_pre / root
            pivot = ahead_pivot - l_next * l_next
            column = ahead - l_col * l_next
            row_pre = ahead_row - l_next * row_k
            l_row = jnp.sum(jnp.where(lane == sub + origin, l_col, 0.0), axis=0, keepdims=True)
            rest = rest - l_col * l_row
            below = jnp.where(sub_col > local, l_col, 0.0)
            solved = jnp.where(sub == local, row_k, solved - below * row_k)
            upper_ref[pl.ds(k, 1), :] = l_row / scale
            return rest, solved, column, pivot, row_pre

        carry = (rest, solved, column, pivot, row_pre)
        rest, solved, column, pivot, row_pre = lax.fori_loop(0, tile, step, carry, unroll=True)
        lower_inv_ref[origin:origin + tile, :] = solved[:tile]
        rest, solved, column = rest[tile:], solved[tile:], column[tile:]
    product = lax.dot_general(
        sketch_ref[...],
        lower_inv_ref[...],
        (((1,), (1,)), ((), ())),
        precision=lax.Precision.HIGHEST,
        preferred_element_type=jnp.float32,
    )
    basis_ref[...] = (product * gain).astype(basis_ref.dtype)


def factor(gram, sketch, scale, gain):
    n = gram.shape[0]
    rows = sketch.shape[0]
    vmem = pl.BlockSpec(memory_space=pltpu.VMEM)
    return pl.pallas_call(
        functools.partial(factor_kernel, scale, gain),
        out_shape=(
            jax.ShapeDtypeStruct((n, n), jnp.float32),
            jax.ShapeDtypeStruct((rows, n), jnp.bfloat16),
        ),
        in_specs=[vmem, vmem],
        out_specs=(vmem, vmem),
        scratch_shapes=[pltpu.VMEM((n, n), jnp.float32)],
        cost_estimate=pl.CostEstimate(
            flops=8 * n * n * n + 12 * rows * n * n,
            bytes_accessed=8 * n * n + 6 * rows * n,
            transcendentals=n,
        ),
    )(gram, sketch)


IND = ("z", "y")
SNP = ("x", "c")


def shards(genotypes, means, scales, basis_in):
    word_rows, snp_cols = genotypes.shape
    zeta = standardize(genotypes, means, scales)
    local_rows = word_rows * 6
    total_rows = local_rows * group_size(IND)
    rank = basis_in.shape[1]
    rows_in = basis_in.reshape(word_rows, 6, rank).transpose(1, 0, 2).reshape(local_rows, rank)
    partial_value = lax.dot_general(
        rows_in, zeta, (((0,), (0,)), ((), ())), preferred_element_type=jnp.float32
    ).T
    loadings = REDUCE_IND(partial_value).astype(jnp.bfloat16)
    sketch_part = jnp.dot(zeta, loadings, preferred_element_type=jnp.float32)
    sketch = REDUCE_SNP(sketch_part)
    gram_local = lax.dot_general(
        sketch, sketch, (((0,), (0,)), ((), ())), precision=lax.Precision.HIGHEST
    )
    gram = REDUCE_IND(gram_local)
    triangle, basis = factor(
        gram, sketch, total_rows * math.sqrt(SNPS), math.sqrt(total_rows)
    )
    basis = basis.reshape(6, word_rows, rank).transpose(1, 0, 2).reshape(local_rows, rank)
    return (basis, triangle)


def butterfly_sum(x, axes):
    for axis in axes:
        size = lax.axis_size(axis)
        distance = 1
        while distance < size:
            pairs = [(i, i ^ distance) for i in range(size)]
            x = x + lax.ppermute(x, axis, pairs)
            distance *= 2
    return x


def group_size(axes):
    size = 1
    for axis in axes:
        size *= lax.axis_size(axis)
    return size


def reduce_scatter(x, axes):
    size = group_size(axes)
    parts = x.reshape(size, x.shape[0] // size, *x.shape[1:])
    return lax.all_to_all(parts, axes, 0, 0, tiled=False).sum(axis=0)


def all_gather(x, axes):
    size = group_size(axes)
    parts = jnp.broadcast_to(x[None], (size,) + x.shape)
    gathered = lax.all_to_all(parts, axes, 0, 0, tiled=False)
    return gathered.reshape(size * x.shape[0], *x.shape[1:])


def REDUCE_IND(x):
    return all_gather(reduce_scatter(x, IND), IND)


def swap_cores(x):
    return lax.ppermute(x, "c", [(0, 1), (1, 0)])


def REDUCE_SNP(x):
    half = x.shape[0] // 2
    core = lax.axis_index("c")
    top, bottom = x[:half], x[half:]
    mine = jnp.where(core == 0, top, bottom) + swap_cores(jnp.where(core == 0, bottom, top))
    mine = all_gather(reduce_scatter(mine, ("x",)), ("x",))
    other = swap_cores(mine)
    top = jnp.where(core == 0, mine, other)
    bottom = jnp.where(core == 0, other, mine)
    return jnp.concatenate([top, bottom], axis=0)


def solution(mesh):
    ind_size, snp_size = mesh.devices.shape
    grid = Mesh(mesh.devices.reshape(8, ind_size // 8, snp_size // 2, 2), ("z", "y", "x", "c"))
    in_specs = (P(IND, SNP), P(SNP), P(SNP), P(IND, None))
    out_specs = (P(IND, None), P())
    return jax.shard_map(shards, mesh=grid, in_specs=in_specs, out_specs=out_specs, check_vma=False)
```

```python
import functools
import math

import jax
import jax.numpy as jnp
from jax import lax
from jax.experimental import pallas as pl
from jax.experimental.pallas import tpu as pltpu
from jax.sharding import Mesh
from jax.sharding import PartitionSpec as P

SNPS = 4096


def standardize(words, means, scales):
    shifts = 2 * jnp.arange(6, dtype=jnp.int32)
    dose = jnp.bitwise_and(jnp.right_shift(words[None, :, :], shifts[:, None, None]), 3)
    values = (dose.astype(jnp.float32) - means) * scales
    return values.astype(jnp.bfloat16).reshape(6 * words.shape[0], words.shape[1])


def factor_kernel(scale, gram_ref, upper_ref, lower_inv_ref):
    n = gram_ref.shape[0]
    tile = 8
    sub_full = lax.broadcasted_iota(jnp.int32, (n, n), 0)
    lane_full = lax.broadcasted_iota(jnp.int32, (n, n), 1)
    rest = gram_ref[...]
    solved = jnp.where(sub_full == lane_full, 1.0, 0.0).astype(jnp.float32)
    column = jnp.sum(jnp.where(lane_full == 0, rest, 0.0), axis=1, keepdims=True)
    pivot = jnp.sum(jnp.where((lane_full == 0) & (sub_full == 0), rest, 0.0), keepdims=True)
    row_pre = solved[0:1, :]
    for origin in range(0, n, tile):
        rows = n - origin
        sub = lax.broadcasted_iota(jnp.int32, (rows, n), 0)
        lane = lax.broadcasted_iota(jnp.int32, (rows, n), 1)
        sub_col = lax.broadcasted_iota(jnp.int32, (rows, 1), 0)

        def step(local, carry, origin=origin, sub=sub, lane=lane, sub_col=sub_col):
            rest, solved, column, pivot, row_pre = carry
            k = origin + local
            root = jnp.sqrt(pivot)
            ahead = jnp.sum(jnp.where(lane == k + 1, rest, 0.0), axis=1, keepdims=True)
            ahead_pivot = jnp.sum(jnp.where(sub_col == local + 1, ahead, 0.0), axis=0, keepdims=True)
            column_next = jnp.sum(jnp.where(sub_col == local + 1, column, 0.0), axis=0, keepdims=True)
            ahead_row = jnp.sum(jnp.where(sub == local + 1, solved, 0.0), axis=0, keepdims=True)
            l_col = jnp.where(sub_col >= local, column / root, 0.0)
            l_next = column_next / root
            row_k = row_pre / root
            pivot = ahead_pivot - l_next * l_next
            column = ahead - l_col * l_next
            row_pre = ahead_row - l_next * row_k
            l_row = jnp.sum(jnp.where(lane == sub + origin, l_col, 0.0), axis=0, keepdims=True)
            rest = rest - l_col * l_row
            below = jnp.where(sub_col > local, l_col, 0.0)
            solved = jnp.where(sub == local, row_k, solved - below * row_k)
            upper_ref[pl.ds(k, 1), :] = l_row / scale
            return rest, solved, column, pivot, row_pre

        carry = (rest, solved, column, pivot, row_pre)
        rest, solved, column, pivot, row_pre = lax.fori_loop(0, tile, step, carry, unroll=True)
        lower_inv_ref[origin:origin + tile, :] = solved[:tile]
        rest, solved, column = rest[tile:], solved[tile:], column[tile:]


def factor(gram, scale):
    n = gram.shape[0]
    vmem = pl.BlockSpec(memory_space=pltpu.VMEM)
    return pl.pallas_call(
        functools.partial(factor_kernel, scale),
        out_shape=(
            jax.ShapeDtypeStruct((n, n), jnp.float32),
            jax.ShapeDtypeStruct((n, n), jnp.float32),
        ),
        in_specs=[vmem],
        out_specs=(vmem, vmem),
        cost_estimate=pl.CostEstimate(
            flops=8 * n * n * n, bytes_accessed=12 * n * n, transcendentals=n
        ),
    )(gram)


IND = ("z", "y")
SNP = ("x", "c")


def shards(genotypes, means, scales, basis_in):
    word_rows, snp_cols = genotypes.shape
    zeta = standardize(genotypes, means, scales)
    local_rows = word_rows * 6
    total_rows = local_rows * group_size(IND)
    rank = basis_in.shape[1]
    rows_in = basis_in.reshape(word_rows, 6, rank).transpose(1, 0, 2).reshape(local_rows, rank)
    partial_value = lax.dot_general(
        rows_in, zeta, (((0,), (0,)), ((), ())), preferred_element_type=jnp.float32
    ).T
    loadings = REDUCE_IND(partial_value).astype(jnp.bfloat16)
    sketch_part = jnp.dot(zeta, loadings, preferred_element_type=jnp.float32)
    mine, other, sketch = REDUCE_SNP(sketch_part)
    gram_local = gram_part(mine) + gram_part(other)
    gram = REDUCE_IND(gram_local)
    triangle, lower_inv = factor(gram, total_rows * math.sqrt(SNPS))
    factor_n = math.sqrt(total_rows)
    basis = (
        lax.dot_general(
            sketch, lower_inv, (((1,), (1,)), ((), ())), precision=lax.Precision.HIGHEST
        )
        * factor_n
    ).astype(jnp.bfloat16)
    basis = basis.reshape(6, word_rows, rank).transpose(1, 0, 2).reshape(local_rows, rank)
    return (basis, triangle)


def butterfly_sum(x, axes):
    for axis in axes:
        size = lax.axis_size(axis)
        distance = 1
        while distance < size:
            pairs = [(i, i ^ distance) for i in range(size)]
            x = x + lax.ppermute(x, axis, pairs)
            distance *= 2
    return x


def group_size(axes):
    size = 1
    for axis in axes:
        size *= lax.axis_size(axis)
    return size


def reduce_scatter(x, axes):
    size = group_size(axes)
    parts = x.reshape(size, x.shape[0] // size, *x.shape[1:])
    return lax.all_to_all(parts, axes, 0, 0, tiled=False).sum(axis=0)


def all_gather(x, axes):
    size = group_size(axes)
    parts = jnp.broadcast_to(x[None], (size,) + x.shape)
    gathered = lax.all_to_all(parts, axes, 0, 0, tiled=False)
    return gathered.reshape(size * x.shape[0], *x.shape[1:])


def REDUCE_IND(x):
    return all_gather(reduce_scatter(x, IND), IND)


def swap_cores(x):
    return lax.ppermute(x, "c", [(0, 1), (1, 0)])


def REDUCE_SNP(x):
    half = x.shape[0] // 2
    core = lax.axis_index("c")
    top, bottom = x[:half], x[half:]
    mine = jnp.where(core == 0, top, bottom) + swap_cores(jnp.where(core == 0, bottom, top))
    mine = all_gather(reduce_scatter(mine, ("x",)), ("x",))
    other = swap_cores(mine)
    top = jnp.where(core == 0, mine, other)
    bottom = jnp.where(core == 0, other, mine)
    return mine, other, jnp.concatenate([top, bottom], axis=0)


def gram_part(rows):
    return lax.dot_general(
        rows, rows, (((0,), (0,)), ((), ())), precision=lax.Precision.HIGHEST
    )


def solution(mesh):
    ind_size, snp_size = mesh.devices.shape
    grid = Mesh(mesh.devices.reshape(8, ind_size // 8, snp_size // 2, 2), ("z", "y", "x", "c"))
    in_specs = (P(IND, SNP), P(SNP), P(SNP), P(IND, None))
    out_specs = (P(IND, None), P())
    return jax.shard_map(shards, mesh=grid, in_specs=in_specs, out_specs=out_specs, check_vma=False)
```

```python
import functools
import math

import jax
import jax.numpy as jnp
from jax import lax
from jax.experimental import pallas as pl
from jax.experimental.pallas import tpu as pltpu
from jax.sharding import Mesh
from jax.sharding import PartitionSpec as P

SNPS = 4096


def standardize(words, means, scales):
    shifts = 2 * jnp.arange(6, dtype=jnp.int32)
    dose = jnp.bitwise_and(jnp.right_shift(words[None, :, :], shifts[:, None, None]), 3)
    values = (dose.astype(jnp.float32) - means) * scales
    return values.astype(jnp.bfloat16).reshape(6 * words.shape[0], words.shape[1])


def factor_kernel(scale, gram_ref, upper_ref, lower_inv_ref):
    n = gram_ref.shape[0]
    tile = 8
    sub_full = lax.broadcasted_iota(jnp.int32, (n, n), 0)
    lane_full = lax.broadcasted_iota(jnp.int32, (n, n), 1)
    rest = gram_ref[...]
    solved = jnp.where(sub_full == lane_full, 1.0, 0.0).astype(jnp.float32)
    column = jnp.sum(jnp.where(lane_full == 0, rest, 0.0), axis=1, keepdims=True)
    pivot = jnp.sum(jnp.where((lane_full == 0) & (sub_full == 0), rest, 0.0), keepdims=True)
    row_pre = solved[0:1, :]
    for origin in range(0, n, tile):
        rows = n - origin
        sub = lax.broadcasted_iota(jnp.int32, (rows, n), 0)
        lane = lax.broadcasted_iota(jnp.int32, (rows, n), 1)
        sub_col = lax.broadcasted_iota(jnp.int32, (rows, 1), 0)

        def step(local, carry, origin=origin, sub=sub, lane=lane, sub_col=sub_col):
            rest, solved, column, pivot, row_pre = carry
            k = origin + local
            root = jnp.sqrt(pivot)
            ahead = jnp.sum(jnp.where(lane == k + 1, rest, 0.0), axis=1, keepdims=True)
            ahead_pivot = jnp.sum(jnp.where(sub_col == local + 1, ahead, 0.0), axis=0, keepdims=True)
            column_next = jnp.sum(jnp.where(sub_col == local + 1, column, 0.0), axis=0, keepdims=True)
            ahead_row = jnp.sum(jnp.where(sub == local + 1, solved, 0.0), axis=0, keepdims=True)
            l_col = jnp.where(sub_col >= local, column / root, 0.0)
            l_next = column_next / root
            row_k = row_pre / root
            pivot = ahead_pivot - l_next * l_next
            column = ahead - l_col * l_next
            row_pre = ahead_row - l_next * row_k
            l_row = jnp.sum(jnp.where(lane == sub + origin, l_col, 0.0), axis=0, keepdims=True)
            rest = rest - l_col * l_row
            below = jnp.where(sub_col > local, l_col, 0.0)
            solved = jnp.where(sub == local, row_k, solved - below * row_k)
            upper_ref[pl.ds(k, 1), :] = l_row / scale
            return rest, solved, column, pivot, row_pre

        carry = (rest, solved, column, pivot, row_pre)
        rest, solved, column, pivot, row_pre = lax.fori_loop(0, tile, step, carry, unroll=True)
        lower_inv_ref[origin:origin + tile, :] = solved[:tile]
        rest, solved, column = rest[tile:], solved[tile:], column[tile:]


def factor(gram, scale):
    n = gram.shape[0]
    vmem = pl.BlockSpec(memory_space=pltpu.VMEM)
    return pl.pallas_call(
        functools.partial(factor_kernel, scale),
        out_shape=(
            jax.ShapeDtypeStruct((n, n), jnp.float32),
            jax.ShapeDtypeStruct((n, n), jnp.float32),
        ),
        in_specs=[vmem],
        out_specs=(vmem, vmem),
        cost_estimate=pl.CostEstimate(
            flops=8 * n * n * n, bytes_accessed=12 * n * n, transcendentals=n
        ),
    )(gram)


IND = ("z", "y")
SNP = ("x", "c")


def shards(genotypes, means, scales, basis_in):
    word_rows, snp_cols = genotypes.shape
    zeta = standardize(genotypes, means, scales)
    local_rows = word_rows * 6
    total_rows = local_rows * group_size(IND)
    rank = basis_in.shape[1]
    rows_in = basis_in.reshape(word_rows, 6, rank).transpose(1, 0, 2).reshape(local_rows, rank)
    partial_value = lax.dot_general(
        rows_in, zeta, (((0,), (0,)), ((), ())), preferred_element_type=jnp.float32
    ).T
    loadings = REDUCE_IND(partial_value).astype(jnp.bfloat16)
    half = local_rows // 2
    core = lax.axis_index("c")
    sent = jnp.dot(
        lax.dynamic_slice_in_dim(zeta, (1 - core) * half, half, 0),
        loadings,
        preferred_element_type=jnp.float32,
    )
    kept = jnp.dot(
        lax.dynamic_slice_in_dim(zeta, core * half, half, 0),
        loadings,
        preferred_element_type=jnp.float32,
    )
    sketch = REDUCE_SNP(lax.optimization_barrier(kept) + swap_cores(sent))
    gram_local = lax.dot_general(
        sketch, sketch, (((0,), (0,)), ((), ())), precision=lax.Precision.HIGHEST
    )
    gram = REDUCE_IND(gram_local)
    triangle, lower_inv = factor(gram, total_rows * math.sqrt(SNPS))
    factor_n = math.sqrt(total_rows)
    basis = (
        lax.dot_general(
            sketch, lower_inv, (((1,), (1,)), ((), ())), precision=lax.Precision.HIGHEST
        )
        * factor_n
    ).astype(jnp.bfloat16)
    basis = basis.reshape(6, word_rows, rank).transpose(1, 0, 2).reshape(local_rows, rank)
    return (basis, triangle)


def butterfly_sum(x, axes):
    for axis in axes:
        size = lax.axis_size(axis)
        distance = 1
        while distance < size:
            pairs = [(i, i ^ distance) for i in range(size)]
            x = x + lax.ppermute(x, axis, pairs)
            distance *= 2
    return x


def group_size(axes):
    size = 1
    for axis in axes:
        size *= lax.axis_size(axis)
    return size


def reduce_scatter(x, axes):
    size = group_size(axes)
    parts = x.reshape(size, x.shape[0] // size, *x.shape[1:])
    return lax.all_to_all(parts, axes, 0, 0, tiled=False).sum(axis=0)


def all_gather(x, axes):
    size = group_size(axes)
    parts = jnp.broadcast_to(x[None], (size,) + x.shape)
    gathered = lax.all_to_all(parts, axes, 0, 0, tiled=False)
    return gathered.reshape(size * x.shape[0], *x.shape[1:])


def REDUCE_IND(x):
    return all_gather(reduce_scatter(x, IND), IND)


def swap_cores(x):
    return lax.ppermute(x, "c", [(0, 1), (1, 0)])


def REDUCE_SNP(x):
    core = lax.axis_index("c")
    mine = all_gather(reduce_scatter(x, ("x",)), ("x",))
    other = swap_cores(mine)
    top = jnp.where(core == 0, mine, other)
    bottom = jnp.where(core == 0, other, mine)
    return jnp.concatenate([top, bottom], axis=0)


def solution(mesh):
    ind_size, snp_size = mesh.devices.shape
    grid = Mesh(mesh.devices.reshape(8, ind_size // 8, snp_size // 2, 2), ("z", "y", "x", "c"))
    in_specs = (P(IND, SNP), P(SNP), P(SNP), P(IND, None))
    out_specs = (P(IND, None), P())
    return jax.shard_map(shards, mesh=grid, in_specs=in_specs, out_specs=out_specs, check_vma=False)
```

```python
import functools
import math

import jax
import jax.numpy as jnp
from jax import lax
from jax.experimental import pallas as pl
from jax.experimental.pallas import tpu as pltpu
from jax.sharding import Mesh
from jax.sharding import PartitionSpec as P

SNPS = 4096


def standardize(words, means, scales):
    shifts = 2 * jnp.arange(6, dtype=jnp.int32)
    dose = jnp.bitwise_and(jnp.right_shift(words[None, :, :], shifts[:, None, None]), 3)
    values = (dose.astype(jnp.float32) - means) * scales
    return values.astype(jnp.bfloat16).reshape(6 * words.shape[0], words.shape[1])


def factor_kernel(scale, gram_ref, upper_ref, lower_inv_ref):
    n = gram_ref.shape[0]
    tile = 8
    sub_full = lax.broadcasted_iota(jnp.int32, (n, n), 0)
    lane_full = lax.broadcasted_iota(jnp.int32, (n, n), 1)
    rest = gram_ref[...]
    solved = jnp.where(sub_full == lane_full, 1.0, 0.0).astype(jnp.float32)
    column = jnp.sum(jnp.where(lane_full == 0, rest, 0.0), axis=1, keepdims=True)
    pivot = jnp.sum(jnp.where((lane_full == 0) & (sub_full == 0), rest, 0.0), keepdims=True)
    row_pre = solved[0:1, :]
    for origin in range(0, n, tile):
        rows = n - origin
        sub = lax.broadcasted_iota(jnp.int32, (rows, n), 0)
        lane = lax.broadcasted_iota(jnp.int32, (rows, n), 1)
        sub_col = lax.broadcasted_iota(jnp.int32, (rows, 1), 0)

        def step(local, carry, origin=origin, sub=sub, lane=lane, sub_col=sub_col):
            rest, solved, column, pivot, row_pre = carry
            k = origin + local
            root = jnp.sqrt(pivot)
            ahead = jnp.sum(jnp.where(lane == k + 1, rest, 0.0), axis=1, keepdims=True)
            ahead_pivot = jnp.sum(jnp.where(sub_col == local + 1, ahead, 0.0), axis=0, keepdims=True)
            column_next = jnp.sum(jnp.where(sub_col == local + 1, column, 0.0), axis=0, keepdims=True)
            ahead_row = jnp.sum(jnp.where(sub == local + 1, solved, 0.0), axis=0, keepdims=True)
            l_col = jnp.where(sub_col >= local, column / root, 0.0)
            l_next = column_next / root
            row_k = row_pre / root
            pivot = ahead_pivot - l_next * l_next
            column = ahead - l_col * l_next
            row_pre = ahead_row - l_next * row_k
            l_row = jnp.sum(jnp.where(lane == sub + origin, l_col, 0.0), axis=0, keepdims=True)
            rest = rest - l_col * l_row
            below = jnp.where(sub_col > local, l_col, 0.0)
            solved = jnp.where(sub == local, row_k, solved - below * row_k)
            upper_ref[pl.ds(k, 1), :] = l_row / scale
            return rest, solved, column, pivot, row_pre

        carry = (rest, solved, column, pivot, row_pre)
        rest, solved, column, pivot, row_pre = lax.fori_loop(0, tile, step, carry, unroll=True)
        lower_inv_ref[origin:origin + tile, :] = solved[:tile]
        rest, solved, column = rest[tile:], solved[tile:], column[tile:]


def factor(gram, scale):
    n = gram.shape[0]
    vmem = pl.BlockSpec(memory_space=pltpu.VMEM)
    return pl.pallas_call(
        functools.partial(factor_kernel, scale),
        out_shape=(
            jax.ShapeDtypeStruct((n, n), jnp.float32),
            jax.ShapeDtypeStruct((n, n), jnp.float32),
        ),
        in_specs=[vmem],
        out_specs=(vmem, vmem),
        cost_estimate=pl.CostEstimate(
            flops=8 * n * n * n, bytes_accessed=12 * n * n, transcendentals=n
        ),
    )(gram)


IND = ("z", "y")
SNP = ("x", "c")


def shards(genotypes, means, scales, basis_in):
    word_rows, snp_cols = genotypes.shape
    zeta = standardize(genotypes, means, scales)
    local_rows = word_rows * 6
    total_rows = local_rows * group_size(IND)
    rank = basis_in.shape[1]
    rows_in = basis_in.reshape(word_rows, 6, rank).transpose(1, 0, 2).reshape(local_rows, rank)
    partial_value = lax.dot_general(
        rows_in, zeta, (((0,), (0,)), ((), ())), preferred_element_type=jnp.float32
    ).T
    loadings = REDUCE_IND(partial_value).astype(jnp.bfloat16)
    half = local_rows // 2
    core = lax.axis_index("c")
    sent = jnp.dot(
        lax.dynamic_slice_in_dim(zeta, (1 - core) * half, half, 0),
        loadings,
        preferred_element_type=jnp.float32,
    )
    kept = jnp.dot(
        lax.dynamic_slice_in_dim(zeta, core * half, half, 0),
        loadings,
        preferred_element_type=jnp.float32,
    )
    mine, other, sketch = REDUCE_SNP(lax.optimization_barrier(kept) + swap_cores(sent))
    gram_local = gram_part(mine) + gram_part(other)
    gram = REDUCE_IND(gram_local)
    triangle, lower_inv = factor(gram, total_rows * math.sqrt(SNPS))
    factor_n = math.sqrt(total_rows)
    basis = (
        lax.dot_general(
            sketch, lower_inv, (((1,), (1,)), ((), ())), precision=lax.Precision.HIGHEST
        )
        * factor_n
    ).astype(jnp.bfloat16)
    basis = basis.reshape(6, word_rows, rank).transpose(1, 0, 2).reshape(local_rows, rank)
    return (basis, triangle)


def butterfly_sum(x, axes):
    for axis in axes:
        size = lax.axis_size(axis)
        distance = 1
        while distance < size:
            pairs = [(i, i ^ distance) for i in range(size)]
            x = x + lax.ppermute(x, axis, pairs)
            distance *= 2
    return x


def group_size(axes):
    size = 1
    for axis in axes:
        size *= lax.axis_size(axis)
    return size


def reduce_scatter(x, axes):
    size = group_size(axes)
    parts = x.reshape(size, x.shape[0] // size, *x.shape[1:])
    return lax.all_to_all(parts, axes, 0, 0, tiled=False).sum(axis=0)


def all_gather(x, axes):
    size = group_size(axes)
    parts = jnp.broadcast_to(x[None], (size,) + x.shape)
    gathered = lax.all_to_all(parts, axes, 0, 0, tiled=False)
    return gathered.reshape(size * x.shape[0], *x.shape[1:])


def REDUCE_IND(x):
    return all_gather(reduce_scatter(x, IND), IND)


def swap_cores(x):
    return lax.ppermute(x, "c", [(0, 1), (1, 0)])


def REDUCE_SNP(x):
    core = lax.axis_index("c")
    mine = all_gather(reduce_scatter(x, ("x",)), ("x",))
    other = swap_cores(mine)
    top = jnp.where(core == 0, mine, other)
    bottom = jnp.where(core == 0, other, mine)
    return mine, other, jnp.concatenate([top, bottom], axis=0)


def gram_part(rows):
    return lax.dot_general(
        rows, rows, (((0,), (0,)), ((), ())), precision=lax.Precision.HIGHEST
    )


def solution(mesh):
    ind_size, snp_size = mesh.devices.shape
    grid = Mesh(mesh.devices.reshape(8, ind_size // 8, snp_size // 2, 2), ("z", "y", "x", "c"))
    in_specs = (P(IND, SNP), P(SNP), P(SNP), P(IND, None))
    out_specs = (P(IND, None), P())
    return jax.shard_map(shards, mesh=grid, in_specs=in_specs, out_specs=out_specs, check_vma=False)
```
